128 devices in a mesh: tx: 8 (over y, x_lo), ty: 16 (over z, x_hi, core).
Axes of the slice: x: 4 (x_hi: 2, x_lo: 2; x = x_hi * 2 + x_lo), y: 4, z: 4, core: 2. Of those that a mesh axis runs over, the one named last changes fastest.
Arguments:
- pressure: float32 [80, 128, 4096], P(None, 'tx', 'ty'), may hold values from -6 to 6
- velocity: float32 [3, 80, 128, 4096], P(None, None, 'tx', 'ty'), may hold values from -6 to 6
- kappa: float32 [80, 128, 4096], P(None, 'tx', 'ty'), may hold values from 0.05 to 0.5
- buoyancy: float32 [3, 80, 128, 4096], P(None, None, 'tx', 'ty'), may hold values from 0.1 to 1
- fwd_pressure: float32 [2, 80, 128, 4096], P(None, None, 'tx', 'ty'), may hold values from -6 to 6
- gradient: float32 [80, 128, 4096], P(None, 'tx', 'ty'), may hold values from -6 to 6
- traces: float32 [131072, 256], P(('tx', 'ty')), may hold values from -6 to 6
- kernel: float32 [2, 256], replicated, may hold values from -0.75 to 0.75
- rec_tile: int32 [131072, 1], P(('tx', 'ty')), may hold values from 0 to 127; in each aligned block of 1024 rows (0 to 1023, 1024 to 2047, ...) at most 16 rows name the same one
- rec_cell: int32 [131072], P(('tx', 'ty')), may hold values from 0 to 4095
Outputs:
- pressure_out: float32 [80, 128, 4096], P(None, 'tx', 'ty')
- velocity_out: float32 [3, 80, 128, 4096], P(None, None, 'tx', 'ty')
- gradient_out: float32 [80, 128, 4096], P(None, 'tx', 'ty')
The draws below stay inside these ranges and needn't reach their ends.
Inputs may be any that keep to these rules, and one draw needn't show every extreme that they name: `rec_tile`: in each aligned block of 1024 rows (the rows of one device) no tile is named by more than 16 rows, a bound that some block reaches.
All inputs are finite; a program needn't handle non-finite values.
Results may differ from the reference program's by a relative error of at most 0.00009.
Values sent between devices are 32-bit elements; how exact they have to be, the bound alone decides.
No kernel may reach another device: no remote copies, remote signals or barrier semaphores. Data moves between devices by JAX's collectives and lax.ppermute only.
A program may use at most 128 MiB of HBM per device.

```python
import math
import jax
import jax.numpy as jnp
import numpy as np
from jax import lax

CX = 16
CY = 256
NZ = 80
NT = 256
STEPS = 2
REC_DEPTH = 3
R_DEV = 1024
CAP = 16
NX = 128
NY = 4096
NREC = 131072
N_TY = 16
DEVICES = 128


def place_ends(values, stream_key, low, high):
    dims = values.shape
    index_at = [jax.random.randint(jax.random.fold_in(stream_key, axis), (), 0, dims[axis]) for axis in range(len(dims))]
    values = values.at[tuple(index_at)].set(low)
    longest = dims.index(max(dims))
    index_at[longest] = (index_at[longest] + 1) % dims[longest]
    return values.at[tuple(index_at)].set(high)


def block_scale(own_key, extent, cuts, least, high):
    def one(axis_at, blocks):
        heights = jax.random.uniform(jax.random.fold_in(jax.random.fold_in(own_key, 6), axis_at), (blocks,), jnp.float32, least / len(cuts), high / len(cuts))
        return jnp.repeat(jnp.exp(heights), extent[axis_at] // blocks).reshape((-1,) + (1,) * (len(extent) - axis_at - 1))

    loudness = one(*cuts[0])
    for cut in cuts[1:]:
        loudness = loudness * one(*cut)
    return loudness


def routed_block(rng, own, number, rows, number_of, top, bound, lean):
    sequence = jax.random.permutation(rng, number_of)
    heavy_load, common = portions_of(number_of, rows * top, bound, lean, True), portions_of(number_of, rows * top, bound, lean, False)
    places = jnp.arange(number_of)

    def named(tallies, turn):
        used = int((tallies > 0).sum())
        fixed = max(1, used // 4)
        shifted = fixed + (places - fixed + turn * (used - fixed)) % max(1, number_of - fixed)
        return jnp.zeros((number_of,), jnp.int32).at[sequence[jnp.where(places < fixed, places, shifted)]].set(jnp.asarray(tallies, jnp.int32))

    tallies = jnp.where(number % 4 == 0, named(heavy_load, number // 4), named(common, number - number // 4 - 1))
    mixed = jax.random.permutation(jax.random.fold_in(own, 3), number_of)
    source_of, taker = mixed[0:number_of // 2 * 2:2], mixed[1:number_of // 2 * 2:2]
    slack = jnp.minimum(tallies[source_of] - 1, bound - tallies[taker]) // 2
    slack = jnp.where((source_of == sequence[0]) | (taker == sequence[0]) | (tallies[taker] == 0), 0, jnp.maximum(slack, 0))
    shifted = jax.random.randint(jax.random.fold_in(own, 4), (number_of // 2,), 0, 1 << 20) % (slack + 1)
    tallies = tallies.at[source_of].add(-shifted).at[taker].add(shifted)
    members = jnp.searchsorted(jnp.cumsum(tallies), jnp.arange(rows * top), side="right").astype(jnp.int32)
    listing = members.reshape(top, rows).T
    listing = listing[jax.random.permutation(jax.random.fold_in(own, 1), rows)]
    turn = jax.random.randint(jax.random.fold_in(own, 2), (rows, 1), 0, top)
    return jnp.take_along_axis(listing, (jnp.arange(top)[None, :] + turn) % top, axis=1)


def portions_of(number_of, total, reach, skew, full):
    loads = [(1 << 20) // math.isqrt(standing ** skew) + 1 for standing in range(1, number_of + 1)]
    largest = reach if full else min(reach, max(-(-total // number_of), total * loads[0] // sum(loads)))
    least = 1 if total - largest >= number_of - 1 else 0
    counts, rest = [largest] + [least] * (number_of - 1), total - largest - least * (number_of - 1)
    while rest > 0:
        candidates = [i for i in range(1, number_of) if counts[i] < largest] or [i for i in range(1, number_of) if counts[i] < reach]
        mass, remaining = sum([loads[i] for i in candidates]), rest
        for i in candidates:
            more = min(reach - counts[i], max(1, remaining * loads[i] // mass), rest)
            counts[i] = counts[i] + more
            rest = rest - more
    return np.array(counts)


def gaussian(stream_key, extent, deviation, bound, pieces=(), held_as=jnp.bfloat16):
    values = jax.random.normal(stream_key, extent, jnp.float32) * deviation
    if len(pieces) > 0:
        values = block_scale(stream_key, extent, pieces, -0.22, 0.18) * values
    return jnp.clip(values, min=-bound, max=bound).astype(held_as)


def setup_inputs(seed: int = 0) -> dict:
    key_of = jax.random.split(jax.random.key(seed), 11)
    pressure = gaussian(key_of[0], (NZ, NX, NY), 1.0, 6.0, ((1, 8), (2, 16)), jnp.float32)
    velocity = gaussian(key_of[1], (3, NZ, NX, NY), 1.0, 6.0, ((2, 8), (3, 16)), jnp.float32)
    kappa = jnp.clip(jnp.exp(math.log(0.5) - 2.3025851 * jax.random.uniform(key_of[2], (NZ, NX, NY), jnp.float32) ** block_scale(key_of[2], (NZ, NX, NY), ((1, 8), (2, 16)), -0.2, 0.2)), 0.05, 0.5)
    buoyancy = jnp.clip(jnp.exp(math.log(1.0) - 2.3025851 * jax.random.uniform(key_of[3], (3, NZ, NX, NY), jnp.float32) ** block_scale(key_of[3], (3, NZ, NX, NY), ((2, 8), (3, 16)), -0.2, 0.2)), 0.1, 1.0)
    fwd_pressure = gaussian(key_of[4], (STEPS, NZ, NX, NY), 1.0, 6.0, ((2, 8), (3, 16)), jnp.float32)
    gradient = gaussian(key_of[5], (NZ, NX, NY), 1.0, 6.0, ((1, 8), (2, 16)), jnp.float32)
    traces = gaussian(key_of[6], (NREC, NT), 1.0, 6.0, ((0, 128),), jnp.float32)
    kernel = gaussian(key_of[7], (STEPS, NT), (NT // 4) ** -0.5, 0.75, (), jnp.float32)
    rec_tile_keys = jax.random.split(jax.random.fold_in(key_of[8], 1), NREC // R_DEV)
    rec_tile_turns = jax.random.permutation(jax.random.fold_in(key_of[8], 3), NREC // R_DEV)
    rec_tile = jax.vmap(lambda own, number: routed_block(jax.random.fold_in(key_of[8], 2), own, number, R_DEV, DEVICES, 1, CAP, 2))(rec_tile_keys, rec_tile_turns).reshape((NREC, 1))
    rec_cell = place_ends(jax.random.randint(key_of[9], (NREC,), 0, CX * CY), jax.random.fold_in(key_of[9], 1), 0, (CX * CY) - 1).astype(jnp.int32)
    return {"pressure": pressure, "velocity": velocity, "kappa": kappa, "buoyancy": buoyancy, "fwd_pressure": fwd_pressure, "gradient": gradient, "traces": traces, "kernel": kernel, "rec_tile": rec_tile, "rec_cell": rec_cell}


coeffs = (1225.0 / 1024.0, -245.0 / 3072.0, 49.0 / 5120.0, -5.0 / 7168.0)


def along(field, axis, start, count):
    return lax.slice_in_dim(field, start, start + count, axis=axis)


def plus_diff(field, axis, count):
    total = coeffs[0] * (along(field, axis, 5, count) - along(field, axis, 4, count))
    for k in range(2, 5):
        total = total + coeffs[k - 1] * (along(field, axis, 4 + k, count) - along(field, axis, 5 - k, count))
    return total


def minus_diff(field, axis, count):
    total = coeffs[0] * (along(field, axis, 4, count) - along(field, axis, 3, count))
    for k in range(2, 5):
        total = total + coeffs[k - 1] * (along(field, axis, 3 + k, count) - along(field, axis, 4 - k, count))
    return total


def reference(pressure, velocity, kappa, buoyancy, fwd_pressure, gradient, traces, kernel, rec_tile, rec_cell):
    nz, nx, ny = pressure.shape
    tiles = rec_tile[:, 0]
    gx = (tiles // N_TY) * CX + rec_cell // CY
    gy = (tiles % N_TY) * CY + rec_cell % CY
    flat = (gx * ny + gy).astype(jnp.int32)
    sources = jnp.einsum("sk,rk->sr", kernel, traces, precision=lax.Precision.HIGHEST)
    inject = jax.ops.segment_sum(sources.T, flat, num_segments=nx * ny)
    inject = inject.T.reshape(STEPS, nx, ny)
    press = pressure
    vel_x, vel_y, vel_z = velocity[0], velocity[1], velocity[2]
    grad = gradient
    for step in range(STEPS):
        padded = jnp.pad(press, ((0, 0), (4, 4), (4, 4)))
        vel_x = vel_x - buoyancy[0] * plus_diff(padded[:, :, 4:4 + ny], 1, nx)
        vel_y = vel_y - buoyancy[1] * plus_diff(padded[:, 4:4 + nx, :], 2, ny)
        zpadded = jnp.pad(press, ((4, 4), (0, 0), (0, 0)))
        vel_z = vel_z - buoyancy[2] * plus_diff(zpadded, 0, nz)
        xpad = jnp.pad(vel_x, ((0, 0), (4, 4), (0, 0)))
        ypad = jnp.pad(vel_y, ((0, 0), (0, 0), (4, 4)))
        zpad = jnp.pad(vel_z, ((4, 4), (0, 0), (0, 0)))
        diverge = minus_diff(xpad, 1, nx) + minus_diff(ypad, 2, ny) + minus_diff(zpad, 0, nz)
        press = press - kappa * diverge
        press = press.at[REC_DEPTH].add(inject[step])
        grad = grad + fwd_pressure[step] * press
    return press, jnp.stack([vel_x, vel_y, vel_z]), grad
```

```python
import functools

import jax
import jax.numpy as jnp
from jax import lax
from jax.experimental import pallas as pl
from jax.experimental.pallas import tpu as pltpu
from jax.sharding import PartitionSpec as P

STEPS = 2
REC_DEPTH = 3
ZC = 4
VMEM_LIMIT = 60 * 1024 * 1024

coeffs = (1225.0 / 1024.0, -245.0 / 3072.0, 49.0 / 5120.0, -5.0 / 7168.0)


def shifted(chunks, s, axis, width):
    if s == 0:
        return jnp.concatenate([chunks[1], chunks[2]], axis=axis)
    idx = lax.broadcasted_iota(jnp.int32, chunks[1].shape, axis)
    if s > 0:
        r = [pltpu.roll(chunks[k], width - s, axis) for k in (1, 2, 3)]
        m = idx < width - s
    else:
        r = [pltpu.roll(chunks[k], -s, axis) for k in (0, 1, 2)]
        m = idx < -s
    return jnp.concatenate([jnp.where(m, r[0], r[1]), jnp.where(m, r[1], r[2])], axis=axis)


def dplus(get):
    total = coeffs[0] * (get(1) - get(0))
    for k in range(2, 5):
        total = total + coeffs[k - 1] * (get(k) - get(1 - k))
    return total


def dminus(get):
    total = coeffs[0] * (get(0) - get(-1))
    for k in range(2, 5):
        total = total + coeffs[k - 1] * (get(k - 1) - get(-k))
    return total


def fill_padded(dst, src_get, nz):
    zeros = jnp.zeros((4,) + dst.shape[1:], jnp.float32)
    dst[0:4] = zeros
    dst[nz + 4 : nz + 8] = zeros

    def fill(i, c):
        z0 = pl.multiple_of(i * ZC, ZC)
        dst[pl.ds(z0 + 4, ZC)] = src_get(pl.ds(z0, ZC))
        return c

    lax.fori_loop(0, nz // ZC, fill, 0)


def vel_kernel(p_ref, pxl_ref, pxh_ref, pyl_ref, pyh_ref, v_ref, b_ref, o_ref, pz_ref):
    nz = p_ref.shape[0]
    fill_padded(pz_ref, lambda zs: p_ref[zs], nz)

    def body(i, c):
        z0 = pl.multiple_of(i * ZC, ZC)
        zs = pl.ds(z0, ZC)
        p = p_ref[zs]
        xch = [pxl_ref[zs], p[:, 0:8, :], p[:, 8:16, :], pxh_ref[zs]]
        o_ref[0, zs] = v_ref[0, zs] - b_ref[0, zs] * dplus(lambda s: shifted(xch, s, 1, 8))
        ych = [pyl_ref[zs], p[:, :, 0:128], p[:, :, 128:256], pyh_ref[zs]]
        o_ref[1, zs] = v_ref[1, zs] - b_ref[1, zs] * dplus(lambda s: shifted(ych, s, 2, 128))
        o_ref[2, zs] = v_ref[2, zs] - b_ref[2, zs] * dplus(
            lambda s: pz_ref[pl.ds(z0 + 4 + s, ZC)]
        )
        return c

    lax.fori_loop(0, nz // ZC, body, 0)


def pres_kernel(
    step, p_ref, v_ref, vxl_ref, vxh_ref, vyl_ref, vyh_ref, k_ref, inj_ref, g_ref, f_ref,
    po_ref, go_ref, vz_ref,
):
    nz = p_ref.shape[0]
    fill_padded(vz_ref, lambda zs: v_ref[2, zs], nz)

    def body(i, c):
        z0 = pl.multiple_of(i * ZC, ZC)
        zs = pl.ds(z0, ZC)
        vx = v_ref[0, zs]
        xch = [vxl_ref[zs], vx[:, 0:8, :], vx[:, 8:16, :], vxh_ref[zs]]
        dx = dminus(lambda s: shifted(xch, s, 1, 8))
        vy = v_ref[1, zs]
        ych = [vyl_ref[zs], vy[:, :, 0:128], vy[:, :, 128:256], vyh_ref[zs]]
        dy = dminus(lambda s: shifted(ych, s, 2, 128))
        dz = dminus(lambda s: vz_ref[pl.ds(z0 + 4 + s, ZC)])
        pn = p_ref[zs] - k_ref[zs] * (dx + dy + dz)
        zid = z0 + lax.broadcasted_iota(jnp.int32, pn.shape, 0)
        pn = jnp.where(zid == REC_DEPTH, pn + inj_ref[...][None], pn)
        po_ref[zs] = pn
        go_ref[zs] = g_ref[zs] + f_ref[step, zs] * pn
        return c

    lax.fori_loop(0, nz // ZC, body, 0)


def vmem_specs(n):
    return [pl.BlockSpec(memory_space=pltpu.VMEM) for _ in range(n)]


def vel_call(p, halos, vel, buoy):
    nz, cx, cy = p.shape
    cells = nz * cx * cy
    return pl.pallas_call(
        vel_kernel,
        out_shape=jax.ShapeDtypeStruct(vel.shape, jnp.float32),
        in_specs=vmem_specs(7),
        out_specs=pl.BlockSpec(memory_space=pltpu.VMEM),
        scratch_shapes=[pltpu.VMEM((nz + 8, cx, cy), jnp.float32)],
        compiler_params=pltpu.CompilerParams(vmem_limit_bytes=VMEM_LIMIT),
        cost_estimate=pl.CostEstimate(
            flops=3 * 26 * cells, bytes_accessed=4 * 11 * cells, transcendentals=0
        ),
    )(p, *halos, vel, buoy)


def pres_call(step, p, vel, halos, kappa, inj, grad, fwd):
    nz, cx, cy = p.shape
    cells = nz * cx * cy
    return pl.pallas_call(
        functools.partial(pres_kernel, step),
        out_shape=(
            jax.ShapeDtypeStruct(p.shape, jnp.float32),
            jax.ShapeDtypeStruct(p.shape, jnp.float32),
        ),
        in_specs=vmem_specs(10),
        out_specs=(
            pl.BlockSpec(memory_space=pltpu.VMEM),
            pl.BlockSpec(memory_space=pltpu.VMEM),
        ),
        scratch_shapes=[pltpu.VMEM((nz + 8, cx, cy), jnp.float32)],
        compiler_params=pltpu.CompilerParams(vmem_limit_bytes=VMEM_LIMIT),
        cost_estimate=pl.CostEstimate(
            flops=3 * 26 * cells + 6 * cells, bytes_accessed=4 * 11 * cells, transcendentals=0
        ),
    )(p, vel, *halos, kappa, inj, grad, fwd)


def neighbours(axis):
    n = lax.axis_size(axis)
    up = [(i, i + 1) for i in range(n - 1)]
    down = [(i + 1, i) for i in range(n - 1)]
    return up, down


def x_halos(f):
    up, down = neighbours("tx")
    cx = f.shape[1]
    lo = lax.ppermute(f[:, cx - 4 :, :], "tx", up)
    hi = lax.ppermute(f[:, :4, :], "tx", down)
    return jnp.pad(lo, ((0, 0), (4, 0), (0, 0))), jnp.pad(hi, ((0, 0), (0, 4), (0, 0)))


def y_halos(f):
    up, down = neighbours("ty")
    cy = f.shape[2]
    lo = lax.ppermute(f[:, :, cy - 4 :], "ty", up)
    hi = lax.ppermute(f[:, :, :4], "ty", down)
    return jnp.pad(lo, ((0, 0), (0, 0), (124, 0))), jnp.pad(hi, ((0, 0), (0, 0), (0, 124)))


def split3(x):
    hi = x.astype(jnp.bfloat16)
    r1 = x - hi.astype(jnp.float32)
    mid = r1.astype(jnp.bfloat16)
    lo = (r1 - mid.astype(jnp.float32)).astype(jnp.bfloat16)
    return [hi, mid, lo]


def receiver_plane(traces, kernel, rec_tile, rec_cell, cx, cy):
    rows = traces.shape[0]
    steps = kernel.shape[0]
    devices = lax.axis_size(("tx", "ty"))
    slots = max(4, 2 * rows // devices)
    tiles = rec_tile[:, 0]
    onehot = (tiles[:, None] == jnp.arange(devices, dtype=jnp.int32)[None, :]).astype(jnp.int32)
    rank = jnp.sum((jnp.cumsum(onehot, axis=0) - 1) * onehot, axis=1)
    slot = tiles * slots + rank
    filtered = jnp.einsum("sk,rk->sr", kernel, traces, precision=lax.Precision.HIGHEST)
    cols = []
    for s in range(steps):
        cols += split3(filtered[s])
    cols += [
        (rec_cell // cy).astype(jnp.bfloat16),
        (rec_cell % cy).astype(jnp.bfloat16),
    ]
    vals = jnp.stack(cols, axis=1)
    place = (
        jnp.arange(devices * slots, dtype=jnp.int32)[:, None] == slot[None, :]
    ).astype(jnp.bfloat16)
    buf = jnp.dot(place, vals, preferred_element_type=jnp.float32)
    send = [buf[:, 3 * s] + buf[:, 3 * s + 1] + buf[:, 3 * s + 2] for s in range(steps)]
    send += [buf[:, 3 * steps], buf[:, 3 * steps + 1]]
    send = jnp.stack(send, axis=0)
    recv = lax.all_to_all(send, ("tx", "ty"), split_axis=1, concat_axis=1, tiled=True)
    rcx, rcy = recv[steps], recv[steps + 1]
    in_row = jnp.arange(cx, dtype=jnp.float32)[:, None] == rcx[None, :]
    lhs = []
    for s in range(steps):
        lhs += split3(jnp.where(in_row, recv[s][None, :], 0.0))
    lhs = jnp.concatenate(lhs, axis=0)
    in_col = (rcy[:, None] == jnp.arange(cy, dtype=jnp.float32)[None, :]).astype(jnp.bfloat16)
    out = jnp.dot(lhs, in_col, preferred_element_type=jnp.float32).reshape(steps, 3, cx, cy)
    return out[:, 0] + out[:, 1] + out[:, 2]


def local(
    pressure, velocity, kappa, buoyancy, fwd_pressure, gradient, traces, kernel, rec_tile, rec_cell
):
    nz, cx, cy = pressure.shape
    inject = receiver_plane(traces, kernel, rec_tile, rec_cell, cx, cy)
    press = pressure
    vel = velocity
    grad = gradient
    for step in range(STEPS):
        ph = x_halos(press) + y_halos(press)
        vel = vel_call(press, ph, vel, buoyancy)
        vh = x_halos(vel[0]) + y_halos(vel[1])
        press, grad = pres_call(step, press, vel, vh, kappa, inject[step], grad, fwd_pressure)
    return press, vel, grad


def solution(mesh):
    return jax.shard_map(
        local,
        mesh=mesh,
        in_specs=(
            P(None, "tx", "ty"),
            P(None, None, "tx", "ty"),
            P(None, "tx", "ty"),
            P(None, None, "tx", "ty"),
            P(None, None, "tx", "ty"),
            P(None, "tx", "ty"),
            P(("tx", "ty"), None),
            P(),
            P(("tx", "ty"), None),
            P(("tx", "ty")),
        ),
        out_specs=(P(None, "tx", "ty"), P(None, None, "tx", "ty"), P(None, "tx", "ty")),
        check_vma=False,
    )
```

```python
import functools

import jax
import jax.numpy as jnp
from jax import lax
from jax.experimental import pallas as pl
from jax.experimental.pallas import tpu as pltpu
from jax.sharding import PartitionSpec as P

STEPS = 2
REC_DEPTH = 3
ZC = 4
ZB = 16
VMEM_LIMIT = 60 * 1024 * 1024

coeffs = (1225.0 / 1024.0, -245.0 / 3072.0, 49.0 / 5120.0, -5.0 / 7168.0)


def shifted(chunks, s, axis, width):
    if s == 0:
        return jnp.concatenate([chunks[1], chunks[2]], axis=axis)
    idx = lax.broadcasted_iota(jnp.int32, chunks[1].shape, axis)
    if s > 0:
        r = [pltpu.roll(chunks[k], width - s, axis) for k in (1, 2, 3)]
        m = idx < width - s
    else:
        r = [pltpu.roll(chunks[k], -s, axis) for k in (0, 1, 2)]
        m = idx < -s
    return jnp.concatenate([jnp.where(m, r[0], r[1]), jnp.where(m, r[1], r[2])], axis=axis)


def dplus(get):
    total = coeffs[0] * (get(1) - get(0))
    for k in range(2, 5):
        total = total + coeffs[k - 1] * (get(k) - get(1 - k))
    return total


def dminus(get):
    total = coeffs[0] * (get(0) - get(-1))
    for k in range(2, 5):
        total = total + coeffs[k - 1] * (get(k - 1) - get(-k))
    return total


def zfill(dst, src_hbm, sem, nz):
    zeros = jnp.zeros((4,) + dst.shape[1:], jnp.float32)
    dst[0:4] = zeros
    dst[nz + 4 : nz + 8] = zeros
    cp = pltpu.make_async_copy(src_hbm, dst.at[pl.ds(4, nz)], sem)
    cp.start()
    cp.wait()


def x_chunks(f, lo_ref, hi_ref, xs, zl):
    xs[0, :, 0:4, :] = lo_ref[pl.ds(zl, ZC)]
    xs[1, :, 0:4, :] = hi_ref[pl.ds(zl, ZC)]
    return [pltpu.roll(xs[0], 4, 1), f[:, 0:8, :], f[:, 8:16, :], xs[1]]


def y_chunks(f, lo_ref, hi_ref, ys, zl):
    ys[0, :, :, 0:4] = lo_ref[pl.ds(zl, ZC)]
    ys[1, :, :, 0:4] = hi_ref[pl.ds(zl, ZC)]
    return [pltpu.roll(ys[0], 124, 2), f[:, :, 0:128], f[:, :, 128:256], ys[1]]


def put_edges(f, zl, top, bot, right, left):
    top[pl.ds(zl, ZC)] = pltpu.roll(f[:, 8:16, :], 4, 1)[:, 0:4, :]
    bot[pl.ds(zl, ZC)] = f[:, 0:4, :]
    right[pl.ds(zl, ZC)] = pltpu.roll(f[:, :, 128:256], 4, 2)[:, :, 0:4]
    left[pl.ds(zl, ZC)] = f[:, :, 0:4]


def vel_kernel(
    p_hbm, pxl, pxh, pyl, pyh, v_ref, b_ref,
    o_ref, vx_top, vx_bot, vy_right, vy_left,
    pz, xs, ys, sem,
):
    nz = p_hbm.shape[0]
    zb = v_ref.shape[1]
    i = pl.program_id(0)

    @pl.when(i == 0)
    def _():
        zfill(pz, p_hbm, sem, nz)

    def body(j, c):
        zl = pl.multiple_of(j * ZC, ZC)
        z0 = pl.multiple_of(i * zb + zl, ZC)
        zs = pl.ds(zl, ZC)
        p = pz[pl.ds(z0 + 4, ZC)]
        xch = x_chunks(p, pxl, pxh, xs, zl)
        vx = v_ref[0, zs] - b_ref[0, zs] * dplus(lambda s: shifted(xch, s, 1, 8))
        o_ref[0, zs] = vx
        ych = y_chunks(p, pyl, pyh, ys, zl)
        vy = v_ref[1, zs] - b_ref[1, zs] * dplus(lambda s: shifted(ych, s, 2, 128))
        o_ref[1, zs] = vy
        o_ref[2, zs] = v_ref[2, zs] - b_ref[2, zs] * dplus(
            lambda s: pz[pl.ds(z0 + 4 + s, ZC)]
        )
        vx_top[zs] = pltpu.roll(vx[:, 8:16, :], 4, 1)[:, 0:4, :]
        vx_bot[zs] = vx[:, 0:4, :]
        vy_right[zs] = pltpu.roll(vy[:, :, 128:256], 4, 2)[:, :, 0:4]
        vy_left[zs] = vy[:, :, 0:4]
        return c

    lax.fori_loop(0, zb // ZC, body, 0)


def pres_kernel(
    p_ref, v_ref, v_hbm, vxl, vxh, vyl, vyh, k_ref, inj_ref, g_ref, f_ref,
    po_ref, go_ref, p_top, p_bot, p_right, p_left,
    vzp, xs, ys, sem,
):
    nz = v_hbm.shape[1]
    zb = p_ref.shape[0]
    i = pl.program_id(0)

    @pl.when(i == 0)
    def _():
        zfill(vzp, v_hbm.at[2], sem, nz)

    def body(j, c):
        zl = pl.multiple_of(j * ZC, ZC)
        z0 = pl.multiple_of(i * zb + zl, ZC)
        zs = pl.ds(zl, ZC)
        xch = x_chunks(v_ref[0, zs], vxl, vxh, xs, zl)
        dx = dminus(lambda s: shifted(xch, s, 1, 8))
        ych = y_chunks(v_ref[1, zs], vyl, vyh, ys, zl)
        dy = dminus(lambda s: shifted(ych, s, 2, 128))
        dz = dminus(lambda s: vzp[pl.ds(z0 + 4 + s, ZC)])
        pn = p_ref[zs] - k_ref[zs] * (dx + dy + dz)
        zid = z0 + lax.broadcasted_iota(jnp.int32, pn.shape, 0)
        pn = jnp.where(zid == REC_DEPTH, pn + inj_ref[...][None], pn)
        po_ref[zs] = pn
        go_ref[zs] = g_ref[zs] + f_ref[zs] * pn
        p_top[zs] = pltpu.roll(pn[:, 8:16, :], 4, 1)[:, 0:4, :]
        p_bot[zs] = pn[:, 0:4, :]
        p_right[zs] = pltpu.roll(pn[:, :, 128:256], 4, 2)[:, :, 0:4]
        p_left[zs] = pn[:, :, 0:4]
        return c

    lax.fori_loop(0, zb // ZC, body, 0)


def scratches(nz, cx, cy):
    return [
        pltpu.VMEM((nz + 8, cx, cy), jnp.float32),
        pltpu.VMEM((2, ZC, 8, cy), jnp.float32),
        pltpu.VMEM((2, ZC, cx, 128), jnp.float32),
        pltpu.SemaphoreType.DMA(()),
    ]


def edge_shapes(nz, cx, cy):
    return [
        jax.ShapeDtypeStruct((nz, 4, cy), jnp.float32),
        jax.ShapeDtypeStruct((nz, 4, cy), jnp.float32),
        jax.ShapeDtypeStruct((nz, cx, 4), jnp.float32),
        jax.ShapeDtypeStruct((nz, cx, 4), jnp.float32),
    ]


def edge_specs(cx, cy):
    return [
        pl.BlockSpec((ZB, 4, cy), lambda i: (i, 0, 0)),
        pl.BlockSpec((ZB, 4, cy), lambda i: (i, 0, 0)),
        pl.BlockSpec((ZB, cx, 4), lambda i: (i, 0, 0)),
        pl.BlockSpec((ZB, cx, 4), lambda i: (i, 0, 0)),
    ]


def vel_call(p, halos, vel, buoy):
    nz, cx, cy = p.shape
    cells = nz * cx * cy
    field3 = pl.BlockSpec((3, ZB, cx, cy), lambda i: (0, i, 0, 0))
    out = pl.pallas_call(
        vel_kernel,
        grid=(nz // ZB,),
        out_shape=[jax.ShapeDtypeStruct(vel.shape, jnp.float32)] + edge_shapes(nz, cx, cy),
        in_specs=[pl.BlockSpec(memory_space=pl.ANY)] + edge_specs(cx, cy) + [field3, field3],
        out_specs=[field3] + edge_specs(cx, cy),
        scratch_shapes=scratches(nz, cx, cy),
        compiler_params=pltpu.CompilerParams(
            vmem_limit_bytes=VMEM_LIMIT, dimension_semantics=("arbitrary",)
        ),
        cost_estimate=pl.CostEstimate(
            flops=3 * 26 * cells, bytes_accessed=4 * 11 * cells, transcendentals=0
        ),
    )(p, *halos, vel, buoy)
    return out[0], tuple(out[1:])


def pres_call(step, p, vel, halos, kappa, inj, grad, fwd):
    nz, cx, cy = p.shape
    cells = nz * cx * cy
    field = pl.BlockSpec((ZB, cx, cy), lambda i: (i, 0, 0))
    out = pl.pallas_call(
        pres_kernel,
        grid=(nz // ZB,),
        out_shape=[
            jax.ShapeDtypeStruct(p.shape, jnp.float32),
            jax.ShapeDtypeStruct(p.shape, jnp.float32),
        ] + edge_shapes(nz, cx, cy),
        in_specs=[
            field,
            pl.BlockSpec((2, ZB, cx, cy), lambda i: (0, i, 0, 0)),
            pl.BlockSpec(memory_space=pl.ANY),
        ] + edge_specs(cx, cy) + [
            field,
            pl.BlockSpec((cx, cy), lambda i: (0, 0)),
            field,
            pl.BlockSpec((None, ZB, cx, cy), lambda i: (step, i, 0, 0)),
        ],
        out_specs=[field, field] + edge_specs(cx, cy),
        scratch_shapes=scratches(nz, cx, cy),
        compiler_params=pltpu.CompilerParams(
            vmem_limit_bytes=VMEM_LIMIT, dimension_semantics=("arbitrary",)
        ),
        cost_estimate=pl.CostEstimate(
            flops=3 * 26 * cells + 6 * cells, bytes_accessed=4 * 10 * cells, transcendentals=0
        ),
    )(p, vel, vel, *halos, kappa, inj, grad, fwd)
    return out[0], out[1], tuple(out[2:])


def neighbours(axis):
    n = lax.axis_size(axis)
    up = [(i, i + 1) for i in range(n - 1)]
    down = [(i + 1, i) for i in range(n - 1)]
    return up, down


def exchange(edges):
    top, bot, right, left = edges
    up_x, down_x = neighbours("tx")
    up_y, down_y = neighbours("ty")
    return (
        lax.ppermute(top, "tx", up_x),
        lax.ppermute(bot, "tx", down_x),
        lax.ppermute(right, "ty", up_y),
        lax.ppermute(left, "ty", down_y),
    )


def edges_of(f):
    cx, cy = f.shape[1], f.shape[2]
    return (f[:, cx - 4 :, :], f[:, :4, :], f[:, :, cy - 4 :], f[:, :, :4])


def split3(x):
    hi = x.astype(jnp.bfloat16)
    r1 = x - hi.astype(jnp.float32)
    mid = r1.astype(jnp.bfloat16)
    lo = (r1 - mid.astype(jnp.float32)).astype(jnp.bfloat16)
    return [hi, mid, lo]


def receiver_plane(traces, kernel, rec_tile, rec_cell, cx, cy):
    rows = traces.shape[0]
    steps = kernel.shape[0]
    devices = lax.axis_size(("tx", "ty"))
    slots = max(4, 2 * rows // devices)
    tiles = rec_tile[:, 0]
    onehot = (tiles[:, None] == jnp.arange(devices, dtype=jnp.int32)[None, :]).astype(jnp.int32)
    rank = jnp.sum((jnp.cumsum(onehot, axis=0) - 1) * onehot, axis=1)
    slot = tiles * slots + rank
    filtered = jnp.einsum("sk,rk->sr", kernel, traces, precision=lax.Precision.HIGHEST)
    cols = []
    for s in range(steps):
        cols += split3(filtered[s])
    cols += [
        (rec_cell // cy).astype(jnp.bfloat16),
        (rec_cell % cy).astype(jnp.bfloat16),
    ]
    vals = jnp.stack(cols, axis=1)
    place = (
        jnp.arange(devices * slots, dtype=jnp.int32)[:, None] == slot[None, :]
    ).astype(jnp.bfloat16)
    buf = jnp.dot(place, vals, preferred_element_type=jnp.float32)
    send = [buf[:, 3 * s] + buf[:, 3 * s + 1] + buf[:, 3 * s + 2] for s in range(steps)]
    send += [buf[:, 3 * steps], buf[:, 3 * steps + 1]]
    send = jnp.stack(send, axis=0)
    recv = lax.all_to_all(send, ("tx", "ty"), split_axis=1, concat_axis=1, tiled=True)
    rcx, rcy = recv[steps], recv[steps + 1]
    in_row = jnp.arange(cx, dtype=jnp.float32)[:, None] == rcx[None, :]
    lhs = []
    for s in range(steps):
        lhs += split3(jnp.where(in_row, recv[s][None, :], 0.0))
    lhs = jnp.concatenate(lhs, axis=0)
    in_col = (rcy[:, None] == jnp.arange(cy, dtype=jnp.float32)[None, :]).astype(jnp.bfloat16)
    out = jnp.dot(lhs, in_col, preferred_element_type=jnp.float32).reshape(steps, 3, cx, cy)
    return out[:, 0] + out[:, 1] + out[:, 2]


def local(
    pressure, velocity, kappa, buoyancy, fwd_pressure, gradient, traces, kernel, rec_tile, rec_cell
):
    nz, cx, cy = pressure.shape
    inject = receiver_plane(traces, kernel, rec_tile, rec_cell, cx, cy)
    press = pressure
    vel = velocity
    grad = gradient
    p_edges = edges_of(pressure)
    for step in range(STEPS):
        vel, v_edges = vel_call(press, exchange(p_edges), vel, buoyancy)
        press, grad, p_edges = pres_call(
            step, press, vel, exchange(v_edges), kappa, inject[step], grad, fwd_pressure
        )
    return press, vel, grad


def solution(mesh):
    return jax.shard_map(
        local,
        mesh=mesh,
        in_specs=(
            P(None, "tx", "ty"),
            P(None, None, "tx", "ty"),
            P(None, "tx", "ty"),
            P(None, None, "tx", "ty"),
            P(None, None, "tx", "ty"),
            P(None, "tx", "ty"),
            P(("tx", "ty"), None),
            P(),
            P(("tx", "ty"), None),
            P(("tx", "ty")),
        ),
        out_specs=(P(None, "tx", "ty"), P(None, None, "tx", "ty"), P(None, "tx", "ty")),
        check_vma=False,
    )
```

```python
import functools

import jax
import jax.numpy as jnp
from jax import lax
from jax.experimental import pallas as pl
from jax.experimental.pallas import tpu as pltpu
from jax.sharding import PartitionSpec as P

STEPS = 2
REC_DEPTH = 3
ZC = 2
ZB = 16
VMEM_LIMIT = 60 * 1024 * 1024

coeffs = (1225.0 / 1024.0, -245.0 / 3072.0, 49.0 / 5120.0, -5.0 / 7168.0)


def shifted(chunks, s, axis, width):
    if s == 0:
        return jnp.concatenate([chunks[1], chunks[2]], axis=axis)
    idx = lax.broadcasted_iota(jnp.int32, chunks[1].shape, axis)
    if s > 0:
        r = [pltpu.roll(chunks[k], width - s, axis) for k in (1, 2, 3)]
        m = idx < width - s
    else:
        r = [pltpu.roll(chunks[k], -s, axis) for k in (0, 1, 2)]
        m = idx < -s
    return jnp.concatenate([jnp.where(m, r[0], r[1]), jnp.where(m, r[1], r[2])], axis=axis)


def dplus(get):
    total = coeffs[0] * (get(1) - get(0))
    for k in range(2, 5):
        total = total + coeffs[k - 1] * (get(k) - get(1 - k))
    return total


def dminus(get):
    total = coeffs[0] * (get(0) - get(-1))
    for k in range(2, 5):
        total = total + coeffs[k - 1] * (get(k - 1) - get(-k))
    return total


def y_chunks(y0, y1, lo_ref, hi_ref, ys, zl):
    ys[0, :, :, 0:4] = lo_ref[pl.ds(zl, ZC)]
    ys[1, :, :, 0:4] = hi_ref[pl.ds(zl, ZC)]
    return [pltpu.roll(ys[0], 124, 2), y0, y1, ys[1]]


def half(h):
    return pl.ds(128 * h, 128)


def vel_kernel(
    p_hbm, pxl, pxh, pyl, pyh, v_ref, b_ref,
    o_ref, vx_top, vx_bot, vy_right, vy_left,
    pz, ys, sem,
):
    nz = p_hbm.shape[0]
    zb = v_ref.shape[1]
    i = pl.program_id(0)

    @pl.when(i == 0)
    def _():
        zeros = jnp.zeros((4,) + pz.shape[1:], jnp.float32)
        pz[0:4] = zeros
        pz[nz + 4 : nz + 8] = zeros
        cps = [
            pltpu.make_async_copy(
                p_hbm.at[:, :, half(h)], pz.at[pl.ds(4, nz), h, pl.ds(8, 16), :], sem.at[h]
            )
            for h in range(2)
        ]
        for cp in cps:
            cp.start()
        for cp in cps:
            cp.wait()

    def body(j, c):
        zl = pl.multiple_of(j * ZC, ZC)
        z0 = pl.multiple_of(i * zb + zl, ZC)
        zs = pl.ds(zl, ZC)
        zp = pl.ds(z0 + 4, ZC)
        for h in range(2):
            pz[zp, h, 4:8, :] = pxl[zs, :, half(h)]
            pz[zp, h, 24:28, :] = pxh[zs, :, half(h)]
        ych = y_chunks(pz[zp, 0, 8:24, :], pz[zp, 1, 8:24, :], pyl, pyh, ys, zl)
        dy = dplus(lambda s: shifted(ych, s, 2, 128))
        for h in range(2):
            dx = dplus(lambda s: pz[zp, h, 8 + s : 24 + s, :])
            vx = v_ref[0, zs, :, half(h)] - b_ref[0, zs, :, half(h)] * dx
            o_ref[0, zs, :, half(h)] = vx
            vx_top[zs, :, half(h)] = pltpu.roll(vx[:, 8:16, :], 4, 1)[:, 0:4, :]
            vx_bot[zs, :, half(h)] = vx[:, 0:4, :]
            vy = v_ref[1, zs, :, half(h)] - b_ref[1, zs, :, half(h)] * dy[:, :, 128 * h : 128 * h + 128]
            o_ref[1, zs, :, half(h)] = vy
            if h == 1:
                vy_right[zs] = pltpu.roll(vy, 4, 2)[:, :, 0:4]
            else:
                vy_left[zs] = vy[:, :, 0:4]
            dz = dplus(lambda s: pz[pl.ds(z0 + 4 + s, ZC), h, 8:24, :])
            o_ref[2, zs, :, half(h)] = v_ref[2, zs, :, half(h)] - b_ref[2, zs, :, half(h)] * dz
        return c

    lax.fori_loop(0, zb // ZC, body, 0)


def pres_kernel(
    p_ref, v_ref, v_hbm, vxl, vxh, vyl, vyh, k_ref, inj_ref, g_ref, f_ref,
    po_ref, go_ref, p_top, p_bot, p_right, p_left,
    vzp, xe, ys, sem,
):
    nz = v_hbm.shape[1]
    zb = p_ref.shape[0]
    i = pl.program_id(0)

    @pl.when(i == 0)
    def _():
        zeros = jnp.zeros((4,) + vzp.shape[1:], jnp.float32)
        vzp[0:4] = zeros
        vzp[nz + 4 : nz + 8] = zeros
        cp = pltpu.make_async_copy(v_hbm.at[2], vzp.at[pl.ds(4, nz)], sem.at[0])
        cp.start()
        cp.wait()

    def body(j, c):
        zl = pl.multiple_of(j * ZC, ZC)
        z0 = pl.multiple_of(i * zb + zl, ZC)
        zs = pl.ds(zl, ZC)
        for h in range(2):
            xe[:, h, 8:24, :] = v_ref[0, zs, :, half(h)]
            xe[:, h, 4:8, :] = vxl[zs, :, half(h)]
            xe[:, h, 24:28, :] = vxh[zs, :, half(h)]
        ych = y_chunks(v_ref[1, zs, :, half(0)], v_ref[1, zs, :, half(1)], vyl, vyh, ys, zl)
        dy = dminus(lambda s: shifted(ych, s, 2, 128))
        zid = z0 + lax.broadcasted_iota(jnp.int32, (ZC, 16, 128), 0)
        for h in range(2):
            dx = dminus(lambda s: xe[:, h, 8 + s : 24 + s, :])
            dz = dminus(lambda s: vzp[pl.ds(z0 + 4 + s, ZC), :, half(h)])
            pn = p_ref[zs, :, half(h)] - k_ref[zs, :, half(h)] * (
                dx + dy[:, :, 128 * h : 128 * h + 128] + dz
            )
            pn = jnp.where(zid == REC_DEPTH, pn + inj_ref[:, half(h)][None], pn)
            po_ref[zs, :, half(h)] = pn
            go_ref[zs, :, half(h)] = g_ref[zs, :, half(h)] + f_ref[zs, :, half(h)] * pn
            p_top[zs, :, half(h)] = pltpu.roll(pn[:, 8:16, :], 4, 1)[:, 0:4, :]
            p_bot[zs, :, half(h)] = pn[:, 0:4, :]
            if h == 1:
                p_right[zs] = pltpu.roll(pn, 4, 2)[:, :, 0:4]
            else:
                p_left[zs] = pn[:, :, 0:4]
        return c

    lax.fori_loop(0, zb // ZC, body, 0)


def edge_shapes(nz, cx, cy):
    return [
        jax.ShapeDtypeStruct((nz, 4, cy), jnp.float32),
        jax.ShapeDtypeStruct((nz, 4, cy), jnp.float32),
        jax.ShapeDtypeStruct((nz, cx, 4), jnp.float32),
        jax.ShapeDtypeStruct((nz, cx, 4), jnp.float32),
    ]


def edge_specs(cx, cy):
    return [
        pl.BlockSpec((ZB, 4, cy), lambda i: (i, 0, 0)),
        pl.BlockSpec((ZB, 4, cy), lambda i: (i, 0, 0)),
        pl.BlockSpec((ZB, cx, 4), lambda i: (i, 0, 0)),
        pl.BlockSpec((ZB, cx, 4), lambda i: (i, 0, 0)),
    ]


def vel_call(p, halos, vel, buoy):
    nz, cx, cy = p.shape
    cells = nz * cx * cy
    field3 = pl.BlockSpec((3, ZB, cx, cy), lambda i: (0, i, 0, 0))
    out = pl.pallas_call(
        vel_kernel,
        grid=(nz // ZB,),
        out_shape=[jax.ShapeDtypeStruct(vel.shape, jnp.float32)] + edge_shapes(nz, cx, cy),
        in_specs=[pl.BlockSpec(memory_space=pl.ANY)] + edge_specs(cx, cy) + [field3, field3],
        out_specs=[field3] + edge_specs(cx, cy),
        scratch_shapes=[
            pltpu.VMEM((nz + 8, 2, 32, 128), jnp.float32),
            pltpu.VMEM((2, ZC, cx, 128), jnp.float32),
            pltpu.SemaphoreType.DMA((2,)),
        ],
        compiler_params=pltpu.CompilerParams(
            vmem_limit_bytes=VMEM_LIMIT, dimension_semantics=("arbitrary",)
        ),
        cost_estimate=pl.CostEstimate(
            flops=3 * 26 * cells, bytes_accessed=4 * 11 * cells, transcendentals=0
        ),
    )(p, *halos, vel, buoy)
    return out[0], tuple(out[1:])


def pres_call(step, p, vel, halos, kappa, inj, grad, fwd):
    nz, cx, cy = p.shape
    cells = nz * cx * cy
    field = pl.BlockSpec((ZB, cx, cy), lambda i: (i, 0, 0))
    out = pl.pallas_call(
        pres_kernel,
        grid=(nz // ZB,),
        out_shape=[
            jax.ShapeDtypeStruct(p.shape, jnp.float32),
            jax.ShapeDtypeStruct(p.shape, jnp.float32),
        ] + edge_shapes(nz, cx, cy),
        in_specs=[
            field,
            pl.BlockSpec((2, ZB, cx, cy), lambda i: (0, i, 0, 0)),
            pl.BlockSpec(memory_space=pl.ANY),
        ] + edge_specs(cx, cy) + [
            field,
            pl.BlockSpec((cx, cy), lambda i: (0, 0)),
            field,
            pl.BlockSpec((None, ZB, cx, cy), lambda i: (step, i, 0, 0)),
        ],
        out_specs=[field, field] + edge_specs(cx, cy),
        scratch_shapes=[
            pltpu.VMEM((nz + 8, cx, cy), jnp.float32),
            pltpu.VMEM((ZC, 2, 32, 128), jnp.float32),
            pltpu.VMEM((2, ZC, cx, 128), jnp.float32),
            pltpu.SemaphoreType.DMA((1,)),
        ],
        compiler_params=pltpu.CompilerParams(
            vmem_limit_bytes=VMEM_LIMIT, dimension_semantics=("arbitrary",)
        ),
        cost_estimate=pl.CostEstimate(
            flops=3 * 26 * cells + 6 * cells, bytes_accessed=4 * 10 * cells, transcendentals=0
        ),
    )(p, vel, vel, *halos, kappa, inj, grad, fwd)
    return out[0], out[1], tuple(out[2:])


def neighbours(axis):
    n = lax.axis_size(axis)
    up = [(i, i + 1) for i in range(n - 1)]
    down = [(i + 1, i) for i in range(n - 1)]
    return up, down


def exchange(edges):
    top, bot, right, left = edges
    up_x, down_x = neighbours("tx")
    up_y, down_y = neighbours("ty")
    return (
        lax.ppermute(top, "tx", up_x),
        lax.ppermute(bot, "tx", down_x),
        lax.ppermute(right, "ty", up_y),
        lax.ppermute(left, "ty", down_y),
    )


def edges_of(f):
    cx, cy = f.shape[1], f.shape[2]
    return (f[:, cx - 4 :, :], f[:, :4, :], f[:, :, cy - 4 :], f[:, :, :4])


def split3(x):
    hi = x.astype(jnp.bfloat16)
    r1 = x - hi.astype(jnp.float32)
    mid = r1.astype(jnp.bfloat16)
    lo = (r1 - mid.astype(jnp.float32)).astype(jnp.bfloat16)
    return [hi, mid, lo]


def receiver_plane(traces, kernel, rec_tile, rec_cell, cx, cy):
    rows = traces.shape[0]
    steps = kernel.shape[0]
    devices = lax.axis_size(("tx", "ty"))
    slots = max(4, 2 * rows // devices)
    tiles = rec_tile[:, 0]
    onehot = (tiles[:, None] == jnp.arange(devices, dtype=jnp.int32)[None, :]).astype(jnp.int32)
    rank = jnp.sum((jnp.cumsum(onehot, axis=0) - 1) * onehot, axis=1)
    slot = tiles * slots + rank
    filtered = jnp.einsum("sk,rk->sr", kernel, traces, precision=lax.Precision.HIGHEST)
    cols = []
    for s in range(steps):
        cols += split3(filtered[s])
    cols += [
        (rec_cell // cy).astype(jnp.bfloat16),
        (rec_cell % cy).astype(jnp.bfloat16),
    ]
    vals = jnp.stack(cols, axis=1)
    place = (
        jnp.arange(devices * slots, dtype=jnp.int32)[:, None] == slot[None, :]
    ).astype(jnp.bfloat16)
    buf = jnp.dot(place, vals, preferred_element_type=jnp.float32)
    send = [buf[:, 3 * s] + buf[:, 3 * s + 1] + buf[:, 3 * s + 2] for s in range(steps)]
    send += [buf[:, 3 * steps], buf[:, 3 * steps + 1]]
    send = jnp.stack(send, axis=0)
    recv = lax.all_to_all(send, ("tx", "ty"), split_axis=1, concat_axis=1, tiled=True)
    rcx, rcy = recv[steps], recv[steps + 1]
    in_row = jnp.arange(cx, dtype=jnp.float32)[:, None] == rcx[None, :]
    lhs = []
    for s in range(steps):
        lhs += split3(jnp.where(in_row, recv[s][None, :], 0.0))
    lhs = jnp.concatenate(lhs, axis=0)
    in_col = (rcy[:, None] == jnp.arange(cy, dtype=jnp.float32)[None, :]).astype(jnp.bfloat16)
    out = jnp.dot(lhs, in_col, preferred_element_type=jnp.float32).reshape(steps, 3, cx, cy)
    return out[:, 0] + out[:, 1] + out[:, 2]


def local(
    pressure, velocity, kappa, buoyancy, fwd_pressure, gradient, traces, kernel, rec_tile, rec_cell
):
    nz, cx, cy = pressure.shape
    inject = receiver_plane(traces, kernel, rec_tile, rec_cell, cx, cy)
    press = pressure
    vel = velocity
    grad = gradient
    p_edges = edges_of(pressure)
    for step in range(STEPS):
        vel, v_edges = vel_call(press, exchange(p_edges), vel, buoyancy)
        press, grad, p_edges = pres_call(
            step, press, vel, exchange(v_edges), kappa, inject[step], grad, fwd_pressure
        )
    return press, vel, grad


def solution(mesh):
    return jax.shard_map(
        local,
        mesh=mesh,
        in_specs=(
            P(None, "tx", "ty"),
            P(None, None, "tx", "ty"),
            P(None, "tx", "ty"),
            P(None, None, "tx", "ty"),
            P(None, None, "tx", "ty"),
            P(None, "tx", "ty"),
            P(("tx", "ty"), None),
            P(),
            P(("tx", "ty"), None),
            P(("tx", "ty")),
        ),
        out_specs=(P(None, "tx", "ty"), P(None, None, "tx", "ty"), P(None, "tx", "ty")),
        check_vma=False,
    )
```

```python
import functools

import jax
import jax.numpy as jnp
from jax import lax
from jax.experimental import pallas as pl
from jax.experimental.pallas import tpu as pltpu
from jax.sharding import PartitionSpec as P

STEPS = 2
REC_DEPTH = 3
ZC = 2
ZB = 16
VMEM_LIMIT = 60 * 1024 * 1024

coeffs = (1225.0 / 1024.0, -245.0 / 3072.0, 49.0 / 5120.0, -5.0 / 7168.0)


def shifted(chunks, s, axis, width):
    if s == 0:
        return jnp.concatenate([chunks[1], chunks[2]], axis=axis)
    idx = lax.broadcasted_iota(jnp.int32, chunks[1].shape, axis)
    if s > 0:
        r = [pltpu.roll(chunks[k], width - s, axis) for k in (1, 2, 3)]
        m = idx < width - s
    else:
        r = [pltpu.roll(chunks[k], -s, axis) for k in (0, 1, 2)]
        m = idx < -s
    return jnp.concatenate([jnp.where(m, r[0], r[1]), jnp.where(m, r[1], r[2])], axis=axis)


def dplus(get):
    total = coeffs[0] * (get(1) - get(0))
    for k in range(2, 5):
        total = total + coeffs[k - 1] * (get(k) - get(1 - k))
    return total


def dminus(get):
    total = coeffs[0] * (get(0) - get(-1))
    for k in range(2, 5):
        total = total + coeffs[k - 1] * (get(k - 1) - get(-k))
    return total


def zfill(dst, src_hbm, sem, nz):
    zeros = jnp.zeros((4,) + dst.shape[1:], jnp.float32)
    dst[0:4] = zeros
    dst[nz + 4 : nz + 8] = zeros
    cp = pltpu.make_async_copy(src_hbm, dst.at[pl.ds(4, nz)], sem)
    cp.start()
    cp.wait()


def x_chunks(f, lo_ref, hi_ref, xs, zl):
    xs[0, :, 0:4, :] = lo_ref[pl.ds(zl, ZC)]
    xs[1, :, 0:4, :] = hi_ref[pl.ds(zl, ZC)]
    return [pltpu.roll(xs[0], 4, 1), f[:, 0:8, :], f[:, 8:16, :], xs[1]]


def y_chunks(f, lo_ref, hi_ref, ys, zl):
    ys[0, :, :, 0:4] = lo_ref[pl.ds(zl, ZC)]
    ys[1, :, :, 0:4] = hi_ref[pl.ds(zl, ZC)]
    return [pltpu.roll(ys[0], 124, 2), f[:, :, 0:128], f[:, :, 128:256], ys[1]]


def put_edges(f, zl, top, bot, right, left):
    top[pl.ds(zl, ZC)] = pltpu.roll(f[:, 8:16, :], 4, 1)[:, 0:4, :]
    bot[pl.ds(zl, ZC)] = f[:, 0:4, :]
    right[pl.ds(zl, ZC)] = pltpu.roll(f[:, :, 128:256], 4, 2)[:, :, 0:4]
    left[pl.ds(zl, ZC)] = f[:, :, 0:4]


def vel_kernel(
    p_hbm, pxl, pxh, pyl, pyh, v_ref, b_ref,
    o_ref, vx_top, vx_bot, vy_right, vy_left,
    pz, xs, ys, sem,
):
    nz = p_hbm.shape[0]
    zb = v_ref.shape[1]
    i = pl.program_id(0)

    @pl.when(i == 0)
    def _():
        zfill(pz, p_hbm, sem, nz)

    def body(j, c):
        zl = pl.multiple_of(j * ZC, ZC)
        z0 = pl.multiple_of(i * zb + zl, ZC)
        zs = pl.ds(zl, ZC)
        p = pz[pl.ds(z0 + 4, ZC)]
        xch = x_chunks(p, pxl, pxh, xs, zl)
        vx = v_ref[0, zs] - b_ref[0, zs] * dplus(lambda s: shifted(xch, s, 1, 8))
        o_ref[0, zs] = vx
        ych = y_chunks(p, pyl, pyh, ys, zl)
        vy = v_ref[1, zs] - b_ref[1, zs] * dplus(lambda s: shifted(ych, s, 2, 128))
        o_ref[1, zs] = vy
        o_ref[2, zs] = v_ref[2, zs] - b_ref[2, zs] * dplus(
            lambda s: pz[pl.ds(z0 + 4 + s, ZC)]
        )
        vx_top[zs] = pltpu.roll(vx[:, 8:16, :], 4, 1)[:, 0:4, :]
        vx_bot[zs] = vx[:, 0:4, :]
        vy_right[zs] = pltpu.roll(vy[:, :, 128:256], 4, 2)[:, :, 0:4]
        vy_left[zs] = vy[:, :, 0:4]
        return c

    lax.fori_loop(0, zb // ZC, body, 0)


def pres_kernel(
    p_ref, v_ref, v_hbm, vxl, vxh, vyl, vyh, k_ref, inj_ref, g_ref, f_ref,
    po_ref, go_ref, p_top, p_bot, p_right, p_left,
    vzp, xs, ys, sem,
):
    nz = v_hbm.shape[1]
    zb = p_ref.shape[0]
    i = pl.program_id(0)

    @pl.when(i == 0)
    def _():
        zfill(vzp, v_hbm.at[2], sem, nz)

    def body(j, c):
        zl = pl.multiple_of(j * ZC, ZC)
        z0 = pl.multiple_of(i * zb + zl, ZC)
        zs = pl.ds(zl, ZC)
        xch = x_chunks(v_ref[0, zs], vxl, vxh, xs, zl)
        dx = dminus(lambda s: shifted(xch, s, 1, 8))
        ych = y_chunks(v_ref[1, zs], vyl, vyh, ys, zl)
        dy = dminus(lambda s: shifted(ych, s, 2, 128))
        dz = dminus(lambda s: vzp[pl.ds(z0 + 4 + s, ZC)])
        pn = p_ref[zs] - k_ref[zs] * (dx + dy + dz)
        zid = z0 + lax.broadcasted_iota(jnp.int32, pn.shape, 0)
        pn = jnp.where(zid == REC_DEPTH, pn + inj_ref[...][None], pn)
        po_ref[zs] = pn
        go_ref[zs] = g_ref[zs] + f_ref[zs] * pn
        p_top[zs] = pltpu.roll(pn[:, 8:16, :], 4, 1)[:, 0:4, :]
        p_bot[zs] = pn[:, 0:4, :]
        p_right[zs] = pltpu.roll(pn[:, :, 128:256], 4, 2)[:, :, 0:4]
        p_left[zs] = pn[:, :, 0:4]
        return c

    lax.fori_loop(0, zb // ZC, body, 0)


def scratches(nz, cx, cy):
    return [
        pltpu.VMEM((nz + 8, cx, cy), jnp.float32),
        pltpu.VMEM((2, ZC, 8, cy), jnp.float32),
        pltpu.VMEM((2, ZC, cx, 128), jnp.float32),
        pltpu.SemaphoreType.DMA(()),
    ]


def edge_shapes(nz, cx, cy):
    return [
        jax.ShapeDtypeStruct((nz, 4, cy), jnp.float32),
        jax.ShapeDtypeStruct((nz, 4, cy), jnp.float32),
        jax.ShapeDtypeStruct((nz, cx, 4), jnp.float32),
        jax.ShapeDtypeStruct((nz, cx, 4), jnp.float32),
    ]


def edge_specs(cx, cy):
    return [
        pl.BlockSpec((ZB, 4, cy), lambda i: (i, 0, 0)),
        pl.BlockSpec((ZB, 4, cy), lambda i: (i, 0, 0)),
        pl.BlockSpec((ZB, cx, 4), lambda i: (i, 0, 0)),
        pl.BlockSpec((ZB, cx, 4), lambda i: (i, 0, 0)),
    ]


def vel_call(p, halos, vel, buoy):
    nz, cx, cy = p.shape
    cells = nz * cx * cy
    field3 = pl.BlockSpec((3, ZB, cx, cy), lambda i: (0, i, 0, 0))
    out = pl.pallas_call(
        vel_kernel,
        grid=(nz // ZB,),
        out_shape=[jax.ShapeDtypeStruct(vel.shape, jnp.float32)] + edge_shapes(nz, cx, cy),
        in_specs=[pl.BlockSpec(memory_space=pl.ANY)] + edge_specs(cx, cy) + [field3, field3],
        out_specs=[field3] + edge_specs(cx, cy),
        scratch_shapes=scratches(nz, cx, cy),
        compiler_params=pltpu.CompilerParams(
            vmem_limit_bytes=VMEM_LIMIT, dimension_semantics=("arbitrary",)
        ),
        cost_estimate=pl.CostEstimate(
            flops=3 * 26 * cells, bytes_accessed=4 * 11 * cells, transcendentals=0
        ),
    )(p, *halos, vel, buoy)
    return out[0], tuple(out[1:])


def pres_call(step, p, vel, halos, kappa, inj, grad, fwd):
    nz, cx, cy = p.shape
    cells = nz * cx * cy
    field = pl.BlockSpec((ZB, cx, cy), lambda i: (i, 0, 0))
    out = pl.pallas_call(
        pres_kernel,
        grid=(nz // ZB,),
        out_shape=[
            jax.ShapeDtypeStruct(p.shape, jnp.float32),
            jax.ShapeDtypeStruct(p.shape, jnp.float32),
        ] + edge_shapes(nz, cx, cy),
        in_specs=[
            field,
            pl.BlockSpec((2, ZB, cx, cy), lambda i: (0, i, 0, 0)),
            pl.BlockSpec(memory_space=pl.ANY),
        ] + edge_specs(cx, cy) + [
            field,
            pl.BlockSpec((cx, cy), lambda i: (0, 0)),
            field,
            pl.BlockSpec((None, ZB, cx, cy), lambda i: (step, i, 0, 0)),
        ],
        out_specs=[field, field] + edge_specs(cx, cy),
        scratch_shapes=scratches(nz, cx, cy),
        compiler_params=pltpu.CompilerParams(
            vmem_limit_bytes=VMEM_LIMIT, dimension_semantics=("arbitrary",)
        ),
        cost_estimate=pl.CostEstimate(
            flops=3 * 26 * cells + 6 * cells, bytes_accessed=4 * 10 * cells, transcendentals=0
        ),
    )(p, vel, vel, *halos, kappa, inj, grad, fwd)
    return out[0], out[1], tuple(out[2:])


def neighbours(axis):
    n = lax.axis_size(axis)
    up = [(i, i + 1) for i in range(n - 1)]
    down = [(i + 1, i) for i in range(n - 1)]
    return up, down


def exchange(edges):
    top, bot, right, left = edges
    up_x, down_x = neighbours("tx")
    up_y, down_y = neighbours("ty")
    return (
        lax.ppermute(top, "tx", up_x),
        lax.ppermute(bot, "tx", down_x),
        lax.ppermute(right, "ty", up_y),
        lax.ppermute(left, "ty", down_y),
    )


def edges_of(f):
    cx, cy = f.shape[1], f.shape[2]
    return (f[:, cx - 4 :, :], f[:, :4, :], f[:, :, cy - 4 :], f[:, :, :4])


def split3(x):
    hi = x.astype(jnp.bfloat16)
    r1 = x - hi.astype(jnp.float32)
    mid = r1.astype(jnp.bfloat16)
    lo = (r1 - mid.astype(jnp.float32)).astype(jnp.bfloat16)
    return [hi, mid, lo]


def receiver_plane(traces, kernel, rec_tile, rec_cell, cx, cy):
    rows = traces.shape[0]
    steps = kernel.shape[0]
    devices = lax.axis_size(("tx", "ty"))
    slots = max(4, 2 * rows // devices)
    tiles = rec_tile[:, 0]
    onehot = (tiles[:, None] == jnp.arange(devices, dtype=jnp.int32)[None, :]).astype(jnp.int32)
    rank = jnp.sum((jnp.cumsum(onehot, axis=0) - 1) * onehot, axis=1)
    slot = tiles * slots + rank
    filtered = jnp.einsum("sk,rk->sr", kernel, traces, precision=lax.Precision.HIGHEST)
    cols = []
    for s in range(steps):
        cols += split3(filtered[s])
    cols += [
        (rec_cell // cy).astype(jnp.bfloat16),
        (rec_cell % cy).astype(jnp.bfloat16),
    ]
    vals = jnp.stack(cols, axis=1)
    place = (
        jnp.arange(devices * slots, dtype=jnp.int32)[:, None] == slot[None, :]
    ).astype(jnp.bfloat16)
    buf = jnp.dot(place, vals, preferred_element_type=jnp.float32)
    send = [buf[:, 3 * s] + buf[:, 3 * s + 1] + buf[:, 3 * s + 2] for s in range(steps)]
    send += [buf[:, 3 * steps], buf[:, 3 * steps + 1]]
    send = jnp.stack(send, axis=0)
    recv = lax.all_to_all(send, ("tx", "ty"), split_axis=1, concat_axis=1, tiled=True)
    rcx, rcy = recv[steps], recv[steps + 1]
    in_row = jnp.arange(cx, dtype=jnp.float32)[:, None] == rcx[None, :]
    lhs = []
    for s in range(steps):
        lhs += split3(jnp.where(in_row, recv[s][None, :], 0.0))
    lhs = jnp.concatenate(lhs, axis=0)
    in_col = (rcy[:, None] == jnp.arange(cy, dtype=jnp.float32)[None, :]).astype(jnp.bfloat16)
    out = jnp.dot(lhs, in_col, preferred_element_type=jnp.float32).reshape(steps, 3, cx, cy)
    return out[:, 0] + out[:, 1] + out[:, 2]


def local(
    pressure, velocity, kappa, buoyancy, fwd_pressure, gradient, traces, kernel, rec_tile, rec_cell
):
    nz, cx, cy = pressure.shape
    inject = receiver_plane(traces, kernel, rec_tile, rec_cell, cx, cy)
    press = pressure
    vel = velocity
    grad = gradient
    p_edges = edges_of(pressure)
    for step in range(STEPS):
        vel, v_edges = vel_call(press, exchange(p_edges), vel, buoyancy)
        press, grad, p_edges = pres_call(
            step, press, vel, exchange(v_edges), kappa, inject[step], grad, fwd_pressure
        )
    return press, vel, grad


def solution(mesh):
    return jax.shard_map(
        local,
        mesh=mesh,
        in_specs=(
            P(None, "tx", "ty"),
            P(None, None, "tx", "ty"),
            P(None, "tx", "ty"),
            P(None, None, "tx", "ty"),
            P(None, None, "tx", "ty"),
            P(None, "tx", "ty"),
            P(("tx", "ty"), None),
            P(),
            P(("tx", "ty"), None),
            P(("tx", "ty")),
        ),
        out_specs=(P(None, "tx", "ty"), P(None, None, "tx", "ty"), P(None, "tx", "ty")),
        check_vma=False,
    )
```

```python
import functools

import jax
import jax.numpy as jnp
from jax import lax
from jax.experimental import pallas as pl
from jax.experimental.pallas import tpu as pltpu
from jax.sharding import PartitionSpec as P

STEPS = 2
REC_DEPTH = 3
ZC = 8
ZB = 16
VMEM_LIMIT = 60 * 1024 * 1024

coeffs = (1225.0 / 1024.0, -245.0 / 3072.0, 49.0 / 5120.0, -5.0 / 7168.0)


def shifted(chunks, s, axis, width):
    if s == 0:
        return jnp.concatenate([chunks[1], chunks[2]], axis=axis)
    idx = lax.broadcasted_iota(jnp.int32, chunks[1].shape, axis)
    if s > 0:
        r = [pltpu.roll(chunks[k], width - s, axis) for k in (1, 2, 3)]
        m = idx < width - s
    else:
        r = [pltpu.roll(chunks[k], -s, axis) for k in (0, 1, 2)]
        m = idx < -s
    return jnp.concatenate([jnp.where(m, r[0], r[1]), jnp.where(m, r[1], r[2])], axis=axis)


def dplus(get):
    total = coeffs[0] * (get(1) - get(0))
    for k in range(2, 5):
        total = total + coeffs[k - 1] * (get(k) - get(1 - k))
    return total


def dminus(get):
    total = coeffs[0] * (get(0) - get(-1))
    for k in range(2, 5):
        total = total + coeffs[k - 1] * (get(k - 1) - get(-k))
    return total


def zfill(dst, src_hbm, sem, nz):
    zeros = jnp.zeros((4,) + dst.shape[1:], jnp.float32)
    dst[0:4] = zeros
    dst[nz + 4 : nz + 8] = zeros
    cp = pltpu.make_async_copy(src_hbm, dst.at[pl.ds(4, nz)], sem)
    cp.start()
    cp.wait()


def x_chunks(f, lo_ref, hi_ref, xs, zl):
    xs[0, :, 0:4, :] = lo_ref[pl.ds(zl, ZC)]
    xs[1, :, 0:4, :] = hi_ref[pl.ds(zl, ZC)]
    return [pltpu.roll(xs[0], 4, 1), f[:, 0:8, :], f[:, 8:16, :], xs[1]]


def y_chunks(f, lo_ref, hi_ref, ys, zl):
    ys[0, :, :, 0:4] = lo_ref[pl.ds(zl, ZC)]
    ys[1, :, :, 0:4] = hi_ref[pl.ds(zl, ZC)]
    return [pltpu.roll(ys[0], 124, 2), f[:, :, 0:128], f[:, :, 128:256], ys[1]]


def put_edges(f, zl, top, bot, right, left):
    top[pl.ds(zl, ZC)] = pltpu.roll(f[:, 8:16, :], 4, 1)[:, 0:4, :]
    bot[pl.ds(zl, ZC)] = f[:, 0:4, :]
    right[pl.ds(zl, ZC)] = pltpu.roll(f[:, :, 128:256], 4, 2)[:, :, 0:4]
    left[pl.ds(zl, ZC)] = f[:, :, 0:4]


def vel_kernel(
    p_hbm, pxl, pxh, pyl, pyh, v_ref, b_ref,
    o_ref, vx_top, vx_bot, vy_right, vy_left,
    pz, xs, ys, sem,
):
    nz = p_hbm.shape[0]
    zb = v_ref.shape[1]
    i = pl.program_id(0)

    @pl.when(i == 0)
    def _():
        zfill(pz, p_hbm, sem, nz)

    def body(j, c):
        zl = pl.multiple_of(j * ZC, ZC)
        z0 = pl.multiple_of(i * zb + zl, ZC)
        zs = pl.ds(zl, ZC)
        p = pz[pl.ds(z0 + 4, ZC)]
        xch = x_chunks(p, pxl, pxh, xs, zl)
        vx = v_ref[0, zs] - b_ref[0, zs] * dplus(lambda s: shifted(xch, s, 1, 8))
        o_ref[0, zs] = vx
        ych = y_chunks(p, pyl, pyh, ys, zl)
        vy = v_ref[1, zs] - b_ref[1, zs] * dplus(lambda s: shifted(ych, s, 2, 128))
        o_ref[1, zs] = vy
        o_ref[2, zs] = v_ref[2, zs] - b_ref[2, zs] * dplus(
            lambda s: pz[pl.ds(z0 + 4 + s, ZC)]
        )
        vx_top[zs] = pltpu.roll(vx[:, 8:16, :], 4, 1)[:, 0:4, :]
        vx_bot[zs] = vx[:, 0:4, :]
        vy_right[zs] = pltpu.roll(vy[:, :, 128:256], 4, 2)[:, :, 0:4]
        vy_left[zs] = vy[:, :, 0:4]
        return c

    lax.fori_loop(0, zb // ZC, body, 0)


def pres_kernel(
    p_ref, v_ref, v_hbm, vxl, vxh, vyl, vyh, k_ref, inj_ref, g_ref, f_ref,
    po_ref, go_ref, p_top, p_bot, p_right, p_left,
    vzp, xs, ys, sem,
):
    nz = v_hbm.shape[1]
    zb = p_ref.shape[0]
    i = pl.program_id(0)

    @pl.when(i == 0)
    def _():
        zfill(vzp, v_hbm.at[2], sem, nz)

    def body(j, c):
        zl = pl.multiple_of(j * ZC, ZC)
        z0 = pl.multiple_of(i * zb + zl, ZC)
        zs = pl.ds(zl, ZC)
        xch = x_chunks(v_ref[0, zs], vxl, vxh, xs, zl)
        dx = dminus(lambda s: shifted(xch, s, 1, 8))
        ych = y_chunks(v_ref[1, zs], vyl, vyh, ys, zl)
        dy = dminus(lambda s: shifted(ych, s, 2, 128))
        dz = dminus(lambda s: vzp[pl.ds(z0 + 4 + s, ZC)])
        pn = p_ref[zs] - k_ref[zs] * (dx + dy + dz)
        zid = z0 + lax.broadcasted_iota(jnp.int32, pn.shape, 0)
        pn = jnp.where(zid == REC_DEPTH, pn + inj_ref[...][None], pn)
        po_ref[zs] = pn
        go_ref[zs] = g_ref[zs] + f_ref[zs] * pn
        p_top[zs] = pltpu.roll(pn[:, 8:16, :], 4, 1)[:, 0:4, :]
        p_bot[zs] = pn[:, 0:4, :]
        p_right[zs] = pltpu.roll(pn[:, :, 128:256], 4, 2)[:, :, 0:4]
        p_left[zs] = pn[:, :, 0:4]
        return c

    lax.fori_loop(0, zb // ZC, body, 0)


def scratches(nz, cx, cy):
    return [
        pltpu.VMEM((nz + 8, cx, cy), jnp.float32),
        pltpu.VMEM((2, ZC, 8, cy), jnp.float32),
        pltpu.VMEM((2, ZC, cx, 128), jnp.float32),
        pltpu.SemaphoreType.DMA(()),
    ]


def edge_shapes(nz, cx, cy):
    return [
        jax.ShapeDtypeStruct((nz, 4, cy), jnp.float32),
        jax.ShapeDtypeStruct((nz, 4, cy), jnp.float32),
        jax.ShapeDtypeStruct((nz, cx, 4), jnp.float32),
        jax.ShapeDtypeStruct((nz, cx, 4), jnp.float32),
    ]


def edge_specs(cx, cy):
    return [
        pl.BlockSpec((ZB, 4, cy), lambda i: (i, 0, 0)),
        pl.BlockSpec((ZB, 4, cy), lambda i: (i, 0, 0)),
        pl.BlockSpec((ZB, cx, 4), lambda i: (i, 0, 0)),
        pl.BlockSpec((ZB, cx, 4), lambda i: (i, 0, 0)),
    ]


def vel_call(p, halos, vel, buoy):
    nz, cx, cy = p.shape
    cells = nz * cx * cy
    field3 = pl.BlockSpec((3, ZB, cx, cy), lambda i: (0, i, 0, 0))
    out = pl.pallas_call(
        vel_kernel,
        grid=(nz // ZB,),
        out_shape=[jax.ShapeDtypeStruct(vel.shape, jnp.float32)] + edge_shapes(nz, cx, cy),
        in_specs=[pl.BlockSpec(memory_space=pl.ANY)] + edge_specs(cx, cy) + [field3, field3],
        out_specs=[field3] + edge_specs(cx, cy),
        scratch_shapes=scratches(nz, cx, cy),
        compiler_params=pltpu.CompilerParams(
            vmem_limit_bytes=VMEM_LIMIT, dimension_semantics=("arbitrary",)
        ),
        cost_estimate=pl.CostEstimate(
            flops=3 * 26 * cells, bytes_accessed=4 * 11 * cells, transcendentals=0
        ),
    )(p, *halos, vel, buoy)
    return out[0], tuple(out[1:])


def pres_call(step, p, vel, halos, kappa, inj, grad, fwd):
    nz, cx, cy = p.shape
    cells = nz * cx * cy
    field = pl.BlockSpec((ZB, cx, cy), lambda i: (i, 0, 0))
    out = pl.pallas_call(
        pres_kernel,
        grid=(nz // ZB,),
        out_shape=[
            jax.ShapeDtypeStruct(p.shape, jnp.float32),
            jax.ShapeDtypeStruct(p.shape, jnp.float32),
        ] + edge_shapes(nz, cx, cy),
        in_specs=[
            field,
            pl.BlockSpec((2, ZB, cx, cy), lambda i: (0, i, 0, 0)),
            pl.BlockSpec(memory_space=pl.ANY),
        ] + edge_specs(cx, cy) + [
            field,
            pl.BlockSpec((cx, cy), lambda i: (0, 0)),
            field,
            pl.BlockSpec((None, ZB, cx, cy), lambda i: (step, i, 0, 0)),
        ],
        out_specs=[field, field] + edge_specs(cx, cy),
        scratch_shapes=scratches(nz, cx, cy),
        compiler_params=pltpu.CompilerParams(
            vmem_limit_bytes=VMEM_LIMIT, dimension_semantics=("arbitrary",)
        ),
        cost_estimate=pl.CostEstimate(
            flops=3 * 26 * cells + 6 * cells, bytes_accessed=4 * 10 * cells, transcendentals=0
        ),
    )(p, vel, vel, *halos, kappa, inj, grad, fwd)
    return out[0], out[1], tuple(out[2:])


def neighbours(axis):
    n = lax.axis_size(axis)
    up = [(i, i + 1) for i in range(n - 1)]
    down = [(i + 1, i) for i in range(n - 1)]
    return up, down


def exchange(edges):
    top, bot, right, left = edges
    up_x, down_x = neighbours("tx")
    up_y, down_y = neighbours("ty")
    return (
        lax.ppermute(top, "tx", up_x),
        lax.ppermute(bot, "tx", down_x),
        lax.ppermute(right, "ty", up_y),
        lax.ppermute(left, "ty", down_y),
    )


def edges_of(f):
    cx, cy = f.shape[1], f.shape[2]
    return (f[:, cx - 4 :, :], f[:, :4, :], f[:, :, cy - 4 :], f[:, :, :4])


def split3(x):
    hi = x.astype(jnp.bfloat16)
    r1 = x - hi.astype(jnp.float32)
    mid = r1.astype(jnp.bfloat16)
    lo = (r1 - mid.astype(jnp.float32)).astype(jnp.bfloat16)
    return [hi, mid, lo]


def receiver_plane(traces, kernel, rec_tile, rec_cell, cx, cy):
    rows = traces.shape[0]
    steps = kernel.shape[0]
    devices = lax.axis_size(("tx", "ty"))
    slots = max(4, 2 * rows // devices)
    tiles = rec_tile[:, 0]
    onehot = (tiles[:, None] == jnp.arange(devices, dtype=jnp.int32)[None, :]).astype(jnp.int32)
    rank = jnp.sum((jnp.cumsum(onehot, axis=0) - 1) * onehot, axis=1)
    slot = tiles * slots + rank
    filtered = jnp.einsum("sk,rk->sr", kernel, traces, precision=lax.Precision.HIGHEST)
    cols = []
    for s in range(steps):
        cols += split3(filtered[s])
    cols += [
        (rec_cell // cy).astype(jnp.bfloat16),
        (rec_cell % cy).astype(jnp.bfloat16),
    ]
    vals = jnp.stack(cols, axis=1)
    place = (
        jnp.arange(devices * slots, dtype=jnp.int32)[:, None] == slot[None, :]
    ).astype(jnp.bfloat16)
    buf = jnp.dot(place, vals, preferred_element_type=jnp.float32)
    send = [buf[:, 3 * s] + buf[:, 3 * s + 1] + buf[:, 3 * s + 2] for s in range(steps)]
    send += [buf[:, 3 * steps], buf[:, 3 * steps + 1]]
    send = jnp.stack(send, axis=0)
    recv = lax.all_to_all(send, ("tx", "ty"), split_axis=1, concat_axis=1, tiled=True)
    rcx, rcy = recv[steps], recv[steps + 1]
    in_row = jnp.arange(cx, dtype=jnp.float32)[:, None] == rcx[None, :]
    lhs = []
    for s in range(steps):
        lhs += split3(jnp.where(in_row, recv[s][None, :], 0.0))
    lhs = jnp.concatenate(lhs, axis=0)
    in_col = (rcy[:, None] == jnp.arange(cy, dtype=jnp.float32)[None, :]).astype(jnp.bfloat16)
    out = jnp.dot(lhs, in_col, preferred_element_type=jnp.float32).reshape(steps, 3, cx, cy)
    return out[:, 0] + out[:, 1] + out[:, 2]


def local(
    pressure, velocity, kappa, buoyancy, fwd_pressure, gradient, traces, kernel, rec_tile, rec_cell
):
    nz, cx, cy = pressure.shape
    inject = receiver_plane(traces, kernel, rec_tile, rec_cell, cx, cy)
    press = pressure
    vel = velocity
    grad = gradient
    p_edges = edges_of(pressure)
    for step in range(STEPS):
        vel, v_edges = vel_call(press, exchange(p_edges), vel, buoyancy)
        press, grad, p_edges = pres_call(
            step, press, vel, exchange(v_edges), kappa, inject[step], grad, fwd_pressure
        )
    return press, vel, grad


def solution(mesh):
    return jax.shard_map(
        local,
        mesh=mesh,
        in_specs=(
            P(None, "tx", "ty"),
            P(None, None, "tx", "ty"),
            P(None, "tx", "ty"),
            P(None, None, "tx", "ty"),
            P(None, None, "tx", "ty"),
            P(None, "tx", "ty"),
            P(("tx", "ty"), None),
            P(),
            P(("tx", "ty"), None),
            P(("tx", "ty")),
        ),
        out_specs=(P(None, "tx", "ty"), P(None, None, "tx", "ty"), P(None, "tx", "ty")),
        check_vma=False,
    )
```

```python
import functools

import jax
import jax.numpy as jnp
from jax import lax
from jax.experimental import pallas as pl
from jax.experimental.pallas import tpu as pltpu
from jax.sharding import PartitionSpec as P

STEPS = 2
REC_DEPTH = 3
ZC = 8
ZB = 16
VMEM_LIMIT = 60 * 1024 * 1024

coeffs = (1225.0 / 1024.0, -245.0 / 3072.0, 49.0 / 5120.0, -5.0 / 7168.0)


def shifted(chunks, s, axis, width):
    if s == 0:
        return jnp.concatenate([chunks[1], chunks[2]], axis=axis)
    idx = lax.broadcasted_iota(jnp.int32, chunks[1].shape, axis)
    if s > 0:
        r = [pltpu.roll(chunks[k], width - s, axis) for k in (1, 2, 3)]
        m = idx < width - s
    else:
        r = [pltpu.roll(chunks[k], -s, axis) for k in (0, 1, 2)]
        m = idx < -s
    return jnp.concatenate([jnp.where(m, r[0], r[1]), jnp.where(m, r[1], r[2])], axis=axis)


def dplus(get):
    total = coeffs[0] * (get(1) - get(0))
    for k in range(2, 5):
        total = total + coeffs[k - 1] * (get(k) - get(1 - k))
    return total


def dminus(get):
    total = coeffs[0] * (get(0) - get(-1))
    for k in range(2, 5):
        total = total + coeffs[k - 1] * (get(k - 1) - get(-k))
    return total


def zfill(dst, src_hbm, sem, nz):
    zeros = jnp.zeros((4,) + dst.shape[1:], jnp.float32)
    dst[0:4] = zeros
    dst[nz + 4 : nz + 8] = zeros
    cp = pltpu.make_async_copy(src_hbm, dst.at[pl.ds(4, nz)], sem)
    cp.start()
    cp.wait()


def x_chunks(f, lo_ref, hi_ref, xs, zl):
    xs[0, :, 0:4, :] = lo_ref[pl.ds(zl, ZC)]
    xs[1, :, 0:4, :] = hi_ref[pl.ds(zl, ZC)]
    return [pltpu.roll(xs[0], 4, 1), f[:, 0:8, :], f[:, 8:16, :], xs[1]]


def y_chunks(f, lo_ref, hi_ref, ys, zl):
    ys[0, :, :, 0:4] = lo_ref[pl.ds(zl, ZC)]
    ys[1, :, :, 0:4] = hi_ref[pl.ds(zl, ZC)]
    return [pltpu.roll(ys[0], 124, 2), f[:, :, 0:128], f[:, :, 128:256], ys[1]]


def put_edges(f, zl, top, bot, right, left):
    top[pl.ds(zl, ZC)] = pltpu.roll(f[:, 8:16, :], 4, 1)[:, 0:4, :]
    bot[pl.ds(zl, ZC)] = f[:, 0:4, :]
    right[pl.ds(zl, ZC)] = pltpu.roll(f[:, :, 128:256], 4, 2)[:, :, 0:4]
    left[pl.ds(zl, ZC)] = f[:, :, 0:4]


def vel_kernel(
    p_hbm, pxl, pxh, pyl, pyh, v_ref, b_ref,
    o_ref, vx_top, vx_bot, vy_right, vy_left,
    pz, xs, ys, sem,
):
    nz = p_hbm.shape[0]
    zb = v_ref.shape[1]
    i = pl.program_id(0)

    @pl.when(i == 0)
    def _():
        zfill(pz, p_hbm, sem, nz)

    def body(j, c):
        zl = pl.multiple_of(j * ZC, ZC)
        z0 = pl.multiple_of(i * zb + zl, ZC)
        zs = pl.ds(zl, ZC)
        p = pz[pl.ds(z0 + 4, ZC)]
        xch = x_chunks(p, pxl, pxh, xs, zl)
        vx = v_ref[0, zs] - b_ref[0, zs] * dplus(lambda s: shifted(xch, s, 1, 8))
        o_ref[0, zs] = vx
        ych = y_chunks(p, pyl, pyh, ys, zl)
        vy = v_ref[1, zs] - b_ref[1, zs] * dplus(lambda s: shifted(ych, s, 2, 128))
        o_ref[1, zs] = vy
        o_ref[2, zs] = v_ref[2, zs] - b_ref[2, zs] * dplus(
            lambda s: pz[pl.ds(z0 + 4 + s, ZC)]
        )
        vx_top[zs] = pltpu.roll(vx[:, 8:16, :], 4, 1)[:, 0:4, :]
        vx_bot[zs] = vx[:, 0:4, :]
        vy_right[zs] = pltpu.roll(vy[:, :, 128:256], 4, 2)[:, :, 0:4]
        vy_left[zs] = vy[:, :, 0:4]
        return c

    lax.fori_loop(0, zb // ZC, body, 0)


def pres_kernel(
    p_ref, v_ref, v_hbm, vxl, vxh, vyl, vyh, k_ref, inj_ref, g_ref, f_ref,
    po_ref, go_ref, p_top, p_bot, p_right, p_left,
    vzp, xs, ys, sem,
):
    nz = v_hbm.shape[1]
    zb = p_ref.shape[0]
    i = pl.program_id(0)

    @pl.when(i == 0)
    def _():
        zfill(vzp, v_hbm.at[2], sem, nz)

    def body(j, c):
        zl = pl.multiple_of(j * ZC, ZC)
        z0 = pl.multiple_of(i * zb + zl, ZC)
        zs = pl.ds(zl, ZC)
        xch = x_chunks(v_ref[0, zs], vxl, vxh, xs, zl)
        dx = dminus(lambda s: shifted(xch, s, 1, 8))
        ych = y_chunks(v_ref[1, zs], vyl, vyh, ys, zl)
        dy = dminus(lambda s: shifted(ych, s, 2, 128))
        dz = dminus(lambda s: vzp[pl.ds(z0 + 4 + s, ZC)])
        pn = p_ref[zs] - k_ref[zs] * (dx + dy + dz)
        zid = z0 + lax.broadcasted_iota(jnp.int32, pn.shape, 0)
        pn = jnp.where(zid == REC_DEPTH, pn + inj_ref[...][None], pn)
        po_ref[zs] = pn
        go_ref[zs] = g_ref[zs] + f_ref[zs] * pn
        p_top[zs] = pltpu.roll(pn[:, 8:16, :], 4, 1)[:, 0:4, :]
        p_bot[zs] = pn[:, 0:4, :]
        p_right[zs] = pltpu.roll(pn[:, :, 128:256], 4, 2)[:, :, 0:4]
        p_left[zs] = pn[:, :, 0:4]
        return c

    lax.fori_loop(0, zb // ZC, body, 0)


def scratches(nz, cx, cy):
    return [
        pltpu.VMEM((nz + 8, cx, cy), jnp.float32),
        pltpu.VMEM((2, ZC, 8, cy), jnp.float32),
        pltpu.VMEM((2, ZC, cx, 128), jnp.float32),
        pltpu.SemaphoreType.DMA(()),
    ]


def edge_shapes(nz, cx, cy):
    return [
        jax.ShapeDtypeStruct((nz, 4, cy), jnp.float32),
        jax.ShapeDtypeStruct((nz, 4, cy), jnp.float32),
        jax.ShapeDtypeStruct((nz, cx, 4), jnp.float32),
        jax.ShapeDtypeStruct((nz, cx, 4), jnp.float32),
    ]


def edge_specs(cx, cy):
    return [
        pl.BlockSpec((ZB, 4, cy), lambda i: (i, 0, 0)),
        pl.BlockSpec((ZB, 4, cy), lambda i: (i, 0, 0)),
        pl.BlockSpec((ZB, cx, 4), lambda i: (i, 0, 0)),
        pl.BlockSpec((ZB, cx, 4), lambda i: (i, 0, 0)),
    ]


def vel_call(p, halos, vel, buoy):
    nz, cx, cy = p.shape
    cells = nz * cx * cy
    field3 = pl.BlockSpec((3, ZB, cx, cy), lambda i: (0, i, 0, 0))
    out = pl.pallas_call(
        vel_kernel,
        grid=(nz // ZB,),
        out_shape=[jax.ShapeDtypeStruct(vel.shape, jnp.float32)] + edge_shapes(nz, cx, cy),
        in_specs=[pl.BlockSpec(memory_space=pl.ANY)] + edge_specs(cx, cy) + [field3, field3],
        out_specs=[field3] + edge_specs(cx, cy),
        scratch_shapes=scratches(nz, cx, cy),
        compiler_params=pltpu.CompilerParams(
            vmem_limit_bytes=VMEM_LIMIT, dimension_semantics=("arbitrary",)
        ),
        cost_estimate=pl.CostEstimate(
            flops=3 * 26 * cells, bytes_accessed=4 * 11 * cells, transcendentals=0
        ),
    )(p, *halos, vel, buoy)
    return out[0], tuple(out[1:])


def pres_call(step, p, vel, halos, kappa, inj, grad, fwd):
    nz, cx, cy = p.shape
    cells = nz * cx * cy
    field = pl.BlockSpec((ZB, cx, cy), lambda i: (i, 0, 0))
    out = pl.pallas_call(
        pres_kernel,
        grid=(nz // ZB,),
        out_shape=[
            jax.ShapeDtypeStruct(p.shape, jnp.float32),
            jax.ShapeDtypeStruct(p.shape, jnp.float32),
        ] + edge_shapes(nz, cx, cy),
        in_specs=[
            field,
            pl.BlockSpec((2, ZB, cx, cy), lambda i: (0, i, 0, 0)),
            pl.BlockSpec(memory_space=pl.ANY),
        ] + edge_specs(cx, cy) + [
            field,
            pl.BlockSpec((cx, cy), lambda i: (0, 0)),
            field,
            pl.BlockSpec((None, ZB, cx, cy), lambda i: (step, i, 0, 0)),
        ],
        out_specs=[field, field] + edge_specs(cx, cy),
        scratch_shapes=scratches(nz, cx, cy),
        compiler_params=pltpu.CompilerParams(
            vmem_limit_bytes=VMEM_LIMIT, dimension_semantics=("arbitrary",)
        ),
        cost_estimate=pl.CostEstimate(
            flops=3 * 26 * cells + 6 * cells, bytes_accessed=4 * 10 * cells, transcendentals=0
        ),
    )(p, vel, vel, *halos, kappa, inj, grad, fwd)
    return out[0], out[1], tuple(out[2:])


def neighbours(axis):
    n = lax.axis_size(axis)
    up = [(i, i + 1) for i in range(n - 1)]
    down = [(i + 1, i) for i in range(n - 1)]
    return up, down


def exchange(edges):
    top, bot, right, left = edges
    up_x, down_x = neighbours("tx")
    up_y, down_y = neighbours("ty")
    return (
        lax.ppermute(top, "tx", up_x),
        lax.ppermute(bot, "tx", down_x),
        lax.ppermute(right, "ty", up_y),
        lax.ppermute(left, "ty", down_y),
    )


def edges_of(f):
    cx, cy = f.shape[1], f.shape[2]
    return (f[:, cx - 4 :, :], f[:, :4, :], f[:, :, cy - 4 :], f[:, :, :4])


def split3(x):
    hi = x.astype(jnp.bfloat16)
    r1 = x - hi.astype(jnp.float32)
    mid = r1.astype(jnp.bfloat16)
    lo = (r1 - mid.astype(jnp.float32)).astype(jnp.bfloat16)
    return [hi, mid, lo]


def receiver_plane(traces, kernel, rec_tile, rec_cell, cx, cy):
    rows = traces.shape[0]
    steps = kernel.shape[0]
    devices = lax.axis_size(("tx", "ty"))
    slots = max(4, 2 * rows // devices)
    tiles = rec_tile[:, 0]
    onehot = (tiles[:, None] == jnp.arange(devices, dtype=jnp.int32)[None, :]).astype(jnp.int32)
    rank = jnp.sum((jnp.cumsum(onehot, axis=0) - 1) * onehot, axis=1)
    slot = tiles * slots + rank
    filtered = jnp.einsum("sk,rk->sr", kernel, traces, precision=lax.Precision.HIGHEST)
    cols = []
    for s in range(steps):
        cols += split3(filtered[s])
    cols += [
        (rec_cell // cy).astype(jnp.bfloat16),
        (rec_cell % cy).astype(jnp.bfloat16),
    ]
    vals = jnp.stack(cols, axis=1)
    place = (
        jnp.arange(devices * slots, dtype=jnp.int32)[:, None] == slot[None, :]
    ).astype(jnp.bfloat16)
    buf = jnp.dot(place, vals, preferred_element_type=jnp.float32)
    send = [buf[:, 3 * s] + buf[:, 3 * s + 1] + buf[:, 3 * s + 2] for s in range(steps)]
    send += [buf[:, 3 * steps], buf[:, 3 * steps + 1]]
    send = jnp.stack(send, axis=0)
    recv = lax.all_to_all(send, ("tx", "ty"), split_axis=1, concat_axis=1, tiled=True)
    rcx, rcy = recv[steps], recv[steps + 1]
    in_row = jnp.arange(cx, dtype=jnp.float32)[:, None] == rcx[None, :]
    lhs = []
    for s in range(steps):
        lhs += split3(jnp.where(in_row, recv[s][None, :], 0.0))
    lhs = jnp.concatenate(lhs, axis=0)
    in_col = (rcy[:, None] == jnp.arange(cy, dtype=jnp.float32)[None, :]).astype(jnp.bfloat16)
    out = jnp.dot(lhs, in_col, preferred_element_type=jnp.float32).reshape(steps, 3, cx, cy)
    return out[:, 0] + out[:, 1] + out[:, 2]


def local(
    pressure, velocity, kappa, buoyancy, fwd_pressure, gradient, traces, kernel, rec_tile, rec_cell
):
    nz, cx, cy = pressure.shape
    press = pressure
    vel = velocity
    grad = gradient
    p_edges = edges_of(pressure)
    inject = None
    for step in range(STEPS):
        vel, v_edges = vel_call(press, exchange(p_edges), vel, buoyancy)
        if inject is None:
            vel, traces, kernel, rec_tile, rec_cell = lax.optimization_barrier(
                (vel, traces, kernel, rec_tile, rec_cell)
            )
            inject = receiver_plane(traces, kernel, rec_tile, rec_cell, cx, cy)
        press, grad, p_edges = pres_call(
            step, press, vel, exchange(v_edges), kappa, inject[step], grad, fwd_pressure
        )
    return press, vel, grad


def solution(mesh):
    return jax.shard_map(
        local,
        mesh=mesh,
        in_specs=(
            P(None, "tx", "ty"),
            P(None, None, "tx", "ty"),
            P(None, "tx", "ty"),
            P(None, None, "tx", "ty"),
            P(None, None, "tx", "ty"),
            P(None, "tx", "ty"),
            P(("tx", "ty"), None),
            P(),
            P(("tx", "ty"), None),
            P(("tx", "ty")),
        ),
        out_specs=(P(None, "tx", "ty"), P(None, None, "tx", "ty"), P(None, "tx", "ty")),
        check_vma=False,
    )
```

```python
import functools

import jax
import jax.numpy as jnp
from jax import lax
from jax.experimental import pallas as pl
from jax.experimental.pallas import tpu as pltpu
from jax.sharding import PartitionSpec as P

STEPS = 2
REC_DEPTH = 3
ZC = 8
ZB = 16
VMEM_LIMIT = 60 * 1024 * 1024

coeffs = (1225.0 / 1024.0, -245.0 / 3072.0, 49.0 / 5120.0, -5.0 / 7168.0)


def shifted(chunks, s, axis, width):
    if s == 0:
        return jnp.concatenate([chunks[1], chunks[2]], axis=axis)
    idx = lax.broadcasted_iota(jnp.int32, chunks[1].shape, axis)
    if s > 0:
        r = [pltpu.roll(chunks[k], width - s, axis) for k in (1, 2, 3)]
        m = idx < width - s
    else:
        r = [pltpu.roll(chunks[k], -s, axis) for k in (0, 1, 2)]
        m = idx < -s
    return jnp.concatenate([jnp.where(m, r[0], r[1]), jnp.where(m, r[1], r[2])], axis=axis)


def dplus(get):
    total = coeffs[0] * (get(1) - get(0))
    for k in range(2, 5):
        total = total + coeffs[k - 1] * (get(k) - get(1 - k))
    return total


def dminus(get):
    total = coeffs[0] * (get(0) - get(-1))
    for k in range(2, 5):
        total = total + coeffs[k - 1] * (get(k - 1) - get(-k))
    return total


def zfill(dst, src_hbm, sem, nz):
    zeros = jnp.zeros((4,) + dst.shape[1:], jnp.float32)
    dst[0:4] = zeros
    dst[nz + 4 : nz + 8] = zeros
    cp = pltpu.make_async_copy(src_hbm, dst.at[pl.ds(4, nz)], sem)
    cp.start()
    cp.wait()


def x_chunks(f, lo_ref, hi_ref, xs, zl):
    xs[0, :, 0:4, :] = lo_ref[pl.ds(zl, ZC)]
    xs[1, :, 0:4, :] = hi_ref[pl.ds(zl, ZC)]
    return [pltpu.roll(xs[0], 4, 1), f[:, 0:8, :], f[:, 8:16, :], xs[1]]


def y_chunks(f, lo_ref, hi_ref, ys, zl):
    ys[0, :, :, 0:4] = lo_ref[pl.ds(zl, ZC)].reshape(ZC, -1, 4)
    ys[1, :, :, 0:4] = hi_ref[pl.ds(zl, ZC)].reshape(ZC, -1, 4)
    return [pltpu.roll(ys[0], 124, 2), f[:, :, 0:128], f[:, :, 128:256], ys[1]]


def vel_kernel(
    p_hbm, pxl, pxh, pyl, pyh, v_ref, b_ref,
    o_ref, vx_top, vx_bot, vy_right, vy_left,
    pz, xs, ys, sem,
):
    nz = p_hbm.shape[0]
    zb = v_ref.shape[1]
    i = pl.program_id(0)

    @pl.when(i == 0)
    def _():
        zfill(pz, p_hbm, sem, nz)

    def body(j, c):
        zl = pl.multiple_of(j * ZC, ZC)
        z0 = pl.multiple_of(i * zb + zl, ZC)
        zs = pl.ds(zl, ZC)
        p = pz[pl.ds(z0 + 4, ZC)]
        xch = x_chunks(p, pxl, pxh, xs, zl)
        vx = v_ref[0, zs] - b_ref[0, zs] * dplus(lambda s: shifted(xch, s, 1, 8))
        o_ref[0, zs] = vx
        ych = y_chunks(p, pyl, pyh, ys, zl)
        vy = v_ref[1, zs] - b_ref[1, zs] * dplus(lambda s: shifted(ych, s, 2, 128))
        o_ref[1, zs] = vy
        o_ref[2, zs] = v_ref[2, zs] - b_ref[2, zs] * dplus(
            lambda s: pz[pl.ds(z0 + 4 + s, ZC)]
        )
        vx_top[zs] = pltpu.roll(vx[:, 8:16, :], 4, 1)[:, 0:4, :]
        vx_bot[zs] = vx[:, 0:4, :]
        vy_right[zs] = pltpu.roll(vy[:, :, 128:256], 4, 2)[:, :, 0:4].reshape(ZC, -1)
        vy_left[zs] = vy[:, :, 0:4].reshape(ZC, -1)
        return c

    lax.fori_loop(0, zb // ZC, body, 0)


def pres_kernel(
    p_ref, v_ref, v_hbm, vxl, vxh, vyl, vyh, k_ref, inj_ref, g_ref, f_ref,
    po_ref, go_ref, p_top, p_bot, p_right, p_left,
    vzp, xs, ys, sem,
):
    nz = v_hbm.shape[1]
    zb = p_ref.shape[0]
    i = pl.program_id(0)

    @pl.when(i == 0)
    def _():
        zfill(vzp, v_hbm.at[2], sem, nz)

    def body(j, c):
        zl = pl.multiple_of(j * ZC, ZC)
        z0 = pl.multiple_of(i * zb + zl, ZC)
        zs = pl.ds(zl, ZC)
        xch = x_chunks(v_ref[0, zs], vxl, vxh, xs, zl)
        dx = dminus(lambda s: shifted(xch, s, 1, 8))
        ych = y_chunks(v_ref[1, zs], vyl, vyh, ys, zl)
        dy = dminus(lambda s: shifted(ych, s, 2, 128))
        dz = dminus(lambda s: vzp[pl.ds(z0 + 4 + s, ZC)])
        pn = p_ref[zs] - k_ref[zs] * (dx + dy + dz)
        zid = z0 + lax.broadcasted_iota(jnp.int32, pn.shape, 0)
        pn = jnp.where(zid == REC_DEPTH, pn + inj_ref[...][None], pn)
        po_ref[zs] = pn
        go_ref[zs] = g_ref[zs] + f_ref[zs] * pn
        p_top[zs] = pltpu.roll(pn[:, 8:16, :], 4, 1)[:, 0:4, :]
        p_bot[zs] = pn[:, 0:4, :]
        p_right[zs] = pltpu.roll(pn[:, :, 128:256], 4, 2)[:, :, 0:4].reshape(ZC, -1)
        p_left[zs] = pn[:, :, 0:4].reshape(ZC, -1)
        return c

    lax.fori_loop(0, zb // ZC, body, 0)


def scratches(nz, cx, cy):
    return [
        pltpu.VMEM((nz + 8, cx, cy), jnp.float32),
        pltpu.VMEM((2, ZC, 8, cy), jnp.float32),
        pltpu.VMEM((2, ZC, cx, 128), jnp.float32),
        pltpu.SemaphoreType.DMA(()),
    ]


def edge_shapes(nz, cx, cy):
    return [
        jax.ShapeDtypeStruct((nz, 4, cy), jnp.float32),
        jax.ShapeDtypeStruct((nz, 4, cy), jnp.float32),
        jax.ShapeDtypeStruct((nz, cx * 4), jnp.float32),
        jax.ShapeDtypeStruct((nz, cx * 4), jnp.float32),
    ]


def edge_specs(cx, cy):
    return [
        pl.BlockSpec((ZB, 4, cy), lambda i: (i, 0, 0)),
        pl.BlockSpec((ZB, 4, cy), lambda i: (i, 0, 0)),
        pl.BlockSpec((ZB, cx * 4), lambda i: (i, 0)),
        pl.BlockSpec((ZB, cx * 4), lambda i: (i, 0)),
    ]


def vel_call(p, halos, vel, buoy):
    nz, cx, cy = p.shape
    cells = nz * cx * cy
    field3 = pl.BlockSpec((3, ZB, cx, cy), lambda i: (0, i, 0, 0))
    out = pl.pallas_call(
        vel_kernel,
        grid=(nz // ZB,),
        out_shape=[jax.ShapeDtypeStruct(vel.shape, jnp.float32)] + edge_shapes(nz, cx, cy),
        in_specs=[pl.BlockSpec(memory_space=pl.ANY)] + edge_specs(cx, cy) + [field3, field3],
        out_specs=[field3] + edge_specs(cx, cy),
        scratch_shapes=scratches(nz, cx, cy),
        compiler_params=pltpu.CompilerParams(
            vmem_limit_bytes=VMEM_LIMIT, dimension_semantics=("arbitrary",)
        ),
        cost_estimate=pl.CostEstimate(
            flops=3 * 26 * cells, bytes_accessed=4 * 11 * cells, transcendentals=0
        ),
    )(p, *halos, vel, buoy)
    return out[0], tuple(out[1:])


def pres_call(step, p, vel, halos, kappa, inj, grad, fwd):
    nz, cx, cy = p.shape
    cells = nz * cx * cy
    field = pl.BlockSpec((ZB, cx, cy), lambda i: (i, 0, 0))
    out = pl.pallas_call(
        pres_kernel,
        grid=(nz // ZB,),
        out_shape=[
            jax.ShapeDtypeStruct(p.shape, jnp.float32),
            jax.ShapeDtypeStruct(p.shape, jnp.float32),
        ] + edge_shapes(nz, cx, cy),
        in_specs=[
            field,
            pl.BlockSpec((2, ZB, cx, cy), lambda i: (0, i, 0, 0)),
            pl.BlockSpec(memory_space=pl.ANY),
        ] + edge_specs(cx, cy) + [
            field,
            pl.BlockSpec((cx, cy), lambda i: (0, 0)),
            field,
            pl.BlockSpec((None, ZB, cx, cy), lambda i: (step, i, 0, 0)),
        ],
        out_specs=[field, field] + edge_specs(cx, cy),
        scratch_shapes=scratches(nz, cx, cy),
        compiler_params=pltpu.CompilerParams(
            vmem_limit_bytes=VMEM_LIMIT, dimension_semantics=("arbitrary",)
        ),
        cost_estimate=pl.CostEstimate(
            flops=3 * 26 * cells + 6 * cells, bytes_accessed=4 * 10 * cells, transcendentals=0
        ),
    )(p, vel, vel, *halos, kappa, inj, grad, fwd)
    return out[0], out[1], tuple(out[2:])


def neighbours(axis):
    n = lax.axis_size(axis)
    up = [(i, i + 1) for i in range(n - 1)]
    down = [(i + 1, i) for i in range(n - 1)]
    return up, down


def exchange(edges):
    top, bot, right, left = edges
    up_x, down_x = neighbours("tx")
    up_y, down_y = neighbours("ty")
    return (
        lax.ppermute(top, "tx", up_x),
        lax.ppermute(bot, "tx", down_x),
        lax.ppermute(right, "ty", up_y),
        lax.ppermute(left, "ty", down_y),
    )


def edges_of(f):
    cx, cy = f.shape[1], f.shape[2]
    nz = f.shape[0]
    return (
        f[:, cx - 4 :, :],
        f[:, :4, :],
        f[:, :, cy - 4 :].reshape(nz, cx * 4),
        f[:, :, :4].reshape(nz, cx * 4),
    )


def split3(x):
    hi = x.astype(jnp.bfloat16)
    r1 = x - hi.astype(jnp.float32)
    mid = r1.astype(jnp.bfloat16)
    lo = (r1 - mid.astype(jnp.float32)).astype(jnp.bfloat16)
    return [hi, mid, lo]


def receiver_plane(traces, kernel, rec_tile, rec_cell, cx, cy):
    rows = traces.shape[0]
    steps = kernel.shape[0]
    devices = lax.axis_size(("tx", "ty"))
    slots = max(4, 2 * rows // devices)
    tiles = rec_tile[:, 0]
    onehot = (tiles[:, None] == jnp.arange(devices, dtype=jnp.int32)[None, :]).astype(jnp.int32)
    rank = jnp.sum((jnp.cumsum(onehot, axis=0) - 1) * onehot, axis=1)
    slot = tiles * slots + rank
    filtered = jnp.einsum("sk,rk->sr", kernel, traces, precision=lax.Precision.HIGHEST)
    cols = []
    for s in range(steps):
        cols += split3(filtered[s])
    cols += [
        (rec_cell // cy).astype(jnp.bfloat16),
        (rec_cell % cy).astype(jnp.bfloat16),
    ]
    vals = jnp.stack(cols, axis=1)
    place = (
        jnp.arange(devices * slots, dtype=jnp.int32)[:, None] == slot[None, :]
    ).astype(jnp.bfloat16)
    buf = jnp.dot(place, vals, preferred_element_type=jnp.float32)
    send = [buf[:, 3 * s] + buf[:, 3 * s + 1] + buf[:, 3 * s + 2] for s in range(steps)]
    send += [buf[:, 3 * steps], buf[:, 3 * steps + 1]]
    send = jnp.stack(send, axis=0)
    recv = lax.all_to_all(send, ("tx", "ty"), split_axis=1, concat_axis=1, tiled=True)
    rcx, rcy = recv[steps], recv[steps + 1]
    in_row = jnp.arange(cx, dtype=jnp.float32)[:, None] == rcx[None, :]
    lhs = []
    for s in range(steps):
        lhs += split3(jnp.where(in_row, recv[s][None, :], 0.0))
    lhs = jnp.concatenate(lhs, axis=0)
    in_col = (rcy[:, None] == jnp.arange(cy, dtype=jnp.float32)[None, :]).astype(jnp.bfloat16)
    out = jnp.dot(lhs, in_col, preferred_element_type=jnp.float32).reshape(steps, 3, cx, cy)
    return out[:, 0] + out[:, 1] + out[:, 2]


def local(
    pressure, velocity, kappa, buoyancy, fwd_pressure, gradient, traces, kernel, rec_tile, rec_cell
):
    nz, cx, cy = pressure.shape
    press = pressure
    vel = velocity
    grad = gradient
    p_edges = edges_of(pressure)
    inject = None
    for step in range(STEPS):
        vel, v_edges = vel_call(press, exchange(p_edges), vel, buoyancy)
        if inject is None:
            vel, traces, kernel, rec_tile, rec_cell = lax.optimization_barrier(
                (vel, traces, kernel, rec_tile, rec_cell)
            )
            inject = receiver_plane(traces, kernel, rec_tile, rec_cell, cx, cy)
        press, grad, p_edges = pres_call(
            step, press, vel, exchange(v_edges), kappa, inject[step], grad, fwd_pressure
        )
    return press, vel, grad


def solution(mesh):
    return jax.shard_map(
        local,
        mesh=mesh,
        in_specs=(
            P(None, "tx", "ty"),
            P(None, None, "tx", "ty"),
            P(None, "tx", "ty"),
            P(None, None, "tx", "ty"),
            P(None, None, "tx", "ty"),
            P(None, "tx", "ty"),
            P(("tx", "ty"), None),
            P(),
            P(("tx", "ty"), None),
            P(("tx", "ty")),
        ),
        out_specs=(P(None, "tx", "ty"), P(None, None, "tx", "ty"), P(None, "tx", "ty")),
        check_vma=False,
    )
```
